32 devices in a mesh: outer: 8 (over z, y), inner: 4 (over x, core).
Axes of the slice: x: 2, y: 2, z: 4, core: 2. Of those that a mesh axis runs over, the one named last changes fastest.
Arguments:
- qkv_blocks: bfloat16 [4096, 16, 512], P(('outer', 'inner')), may hold values from -4 to 4
- block_scales: bfloat16 [128, 16, 4], P(('outer', 'inner')), may hold values from 0.25 to 4
- gate_logits: bfloat16 [4096, 16, 4], P(('outer', 'inner')), may hold values from -5 to 45056
- conv_weight: float32 [4, 16, 512], P(None, 'inner'), may hold values from -3 to 3
- decay_log: float32 [32], P('inner'), may hold values from -15 to -3
- dt_bias: float32 [32], P('inner'), may hold values from -1 to 1
- norm_gain: float32 [128], replicated, may hold values from 0.5 to 1.5
Outputs:
- normed_heads: bfloat16 [4096, 32, 128], P(('outer', 'inner'))
The draws below stay inside these ranges and needn't reach their ends.
All inputs are finite; a program needn't handle non-finite values.
Results may differ from the reference program's by a relative error of at most 0.0004.
Values may be sent and summed in bfloat16 or wider, within the bound.
No kernel may reach another device: no remote copies, remote signals or barrier semaphores. Data moves between devices by JAX's collectives and lax.ppermute only.
A program may use at most 128 MiB of HBM per device.

```python
import math
import jax
import jax.numpy as jnp
from jax import lax

HK = 16
HD = 128
VALUE_HEADS = 32
BLOCK = 128
QB = 32
CONV = 4
SEQUENCE_TOKENS = 4096


def decay_plan(key):
    full_key_rows = jax.random.split(jax.random.fold_in(key, 7301), 8)
    head_kind = jax.random.randint(full_key_rows[0], (VALUE_HEADS,), 0, 8)
    slow_rate = 0.15 / SEQUENCE_TOKENS * jnp.exp(jax.random.uniform(full_key_rows[1], (VALUE_HEADS,), jnp.float32, 0.0, math.log(2.0)))
    fast_rate = jnp.exp(jax.random.uniform(full_key_rows[2], (VALUE_HEADS,), jnp.float32, math.log(1.0 / 50.0), math.log(1.0 / 30.0)))
    middle_rate = jnp.exp(jax.random.uniform(full_key_rows[3], (VALUE_HEADS,), jnp.float32, math.log(1.0 / (16.0 * BLOCK)), math.log(1.0 / 60.0)))
    per_head_decay_rate = jnp.where(head_kind < 4, slow_rate, jnp.where(head_kind < 6, middle_rate, fast_rate))
    shift_bias = jax.random.uniform(full_key_rows[4], (VALUE_HEADS,), jnp.float32, -1.0, 1.0)
    spike_position = jax.random.randint(full_key_rows[5], (3,), 0, SEQUENCE_TOKENS)
    spike_decay_drop = jax.random.uniform(full_key_rows[6], (3, VALUE_HEADS), jnp.float32, 0.2, 0.4)
    rate_spread_range = jnp.exp(jax.random.uniform(full_key_rows[7], (SEQUENCE_TOKENS, VALUE_HEADS), jnp.float32, math.log(0.5), math.log(2.0)))
    token_position = jnp.arange(SEQUENCE_TOKENS, dtype=jnp.int32)
    spike_decay_rate = jnp.zeros((SEQUENCE_TOKENS, VALUE_HEADS), jnp.float32)
    spike_applied = jnp.zeros((SEQUENCE_TOKENS,), jnp.bool_)
    for block_number in range(3):
        spike_token_mask = token_position == spike_position[block_number]
        spike_decay_rate = spike_decay_rate + jnp.where(spike_token_mask[:, None], -jnp.log1p(-spike_decay_drop[block_number])[None, :], 0.0)
        spike_applied = jnp.logical_or(spike_applied, spike_token_mask)
    target_values = jnp.where(spike_applied[:, None], spike_decay_rate / per_head_decay_rate[None, :], rate_spread_range)
    inverse = target_values + jnp.log(-jnp.expm1(-target_values))
    return (jnp.log(per_head_decay_rate), shift_bias, inverse - shift_bias[None, :])


def draw_decay_log(key, part):
    return decay_plan(key)[0]


def draw_dt_bias(key, part):
    return decay_plan(key)[1]


def draw_gate_logits(key, part):
    plan = decay_plan(key)
    beta_key = jax.random.fold_in(key, 4409)
    beta_logit = jnp.clip(-2.5 + jax.random.normal(beta_key, (SEQUENCE_TOKENS, VALUE_HEADS), jnp.float32), -5.0, 0.0)
    joined = jnp.concatenate([beta_logit.reshape(SEQUENCE_TOKENS, HK, 2), plan[2].reshape(SEQUENCE_TOKENS, HK, 2)], axis=2)
    return joined.astype(jnp.bfloat16)


def block_scale(key, extent, cuts, low, high):
    gain = 1.0
    for position, shards_of in cuts:
        heights = jax.random.uniform(jax.random.fold_in(jax.random.fold_in(key, 6), position), (shards_of,), jnp.float32, low / len(cuts), high / len(cuts))
        gain = gain * jnp.repeat(jnp.exp(heights), extent[position] // shards_of).reshape((-1,) + (1,) * (len(extent) - 1 - position))
    return gain


def scatter_about(key, extent, spread, reach, cuts=(), held_as=jnp.bfloat16):
    factor_of = block_scale(key, extent, cuts, -0.22, 0.18) if cuts else 1.0
    array = jax.random.normal(key, extent, jnp.float32) * spread * factor_of
    return jnp.minimum(jnp.maximum(array, -reach), reach).astype(held_as)


def setup_inputs(seed: int = 0) -> dict:
    key_list = jax.random.split(jax.random.key(seed), 8)
    return {
        "qkv_blocks": scatter_about(key_list[0], (SEQUENCE_TOKENS, HK, 4 * HD), 1.0, 4.0, ((0, 32),)),
        "block_scales": jnp.clip(jnp.exp(math.log(4.0) - 2.7725887 * jax.random.uniform(key_list[1], (SEQUENCE_TOKENS // QB, HK, 4), jnp.float32) ** block_scale(key_list[1], (SEQUENCE_TOKENS // QB, HK, 4), ((0, 32),), -0.2, 0.2)), 0.25, 4.0).astype(jnp.bfloat16),
        "gate_logits": draw_gate_logits(jax.random.fold_in(key_list[7], 71), 0),
        "conv_weight": scatter_about(key_list[3], (CONV, HK, 4 * HD), 0.5, 3.0, ((1, 4),), jnp.float32),
        "decay_log": draw_decay_log(jax.random.fold_in(key_list[7], 71), 0),
        "dt_bias": draw_dt_bias(jax.random.fold_in(key_list[7], 71), 0),
        "norm_gain": jnp.clip(1.0 + 0.1 * jax.random.normal(key_list[6], (HD,), jnp.float32), 0.5, 1.5),
    }


HIGH_PRECISION = lax.Precision.HIGHEST
EPS_NORM = 1e-06

def dequantize(blocks, scales):
    token_count = blocks.shape[0]
    head_count = blocks.shape[1]
    quarter = blocks.shape[2] // 4
    shaped = blocks.astype(jnp.float32).reshape(token_count // QB, QB, head_count, 4, quarter)
    scaled = shaped * scales.astype(jnp.float32)[:, None, :, :, None]
    return scaled.reshape(token_count, head_count, 4 * quarter)

def convolve(extended, conv_weight, token_count):
    summed = conv_weight[0] * extended[0:token_count]
    for offset in range(1, CONV):
        summed = summed + conv_weight[offset] * extended[offset:offset + token_count]
    return jax.nn.silu(summed)

def unit_rows(matrix):
    return matrix * lax.rsqrt(lax.optimization_barrier(jnp.sum(matrix * matrix, axis=-1, keepdims=True)) + EPS_NORM)

def split_heads(mixed, gate_now, decay_log, dt_bias):
    token_count = mixed.shape[0]
    value_heads = 2 * mixed.shape[1]
    queries = jnp.repeat(unit_rows(mixed[:, :, :HD]), 2, axis=1)
    keys_in = jnp.repeat(unit_rows(mixed[:, :, HD:2 * HD]), 2, axis=1)
    values_in = mixed[:, :, 2 * HD:].reshape(token_count, value_heads, HD)
    gate_values = gate_now.astype(jnp.float32)
    beta_gate = jax.nn.sigmoid(gate_values[:, :, :2].reshape(token_count, value_heads))
    raw_decay = gate_values[:, :, 2:].reshape(token_count, value_heads)
    log_decay = -jnp.exp(decay_log) * jax.nn.softplus(raw_decay + dt_bias)
    return (jnp.swapaxes(queries, 0, 1), jnp.swapaxes(keys_in, 0, 1), jnp.swapaxes(values_in, 0, 1), jnp.swapaxes(beta_gate, 0, 1), jnp.swapaxes(log_decay, 0, 1))

def block_terms(queries, keys_in, values_in, beta_gate, log_decay):
    cumulative = jnp.cumsum(log_decay, axis=-1)
    length = log_decay.shape[-1]
    row_index = lax.broadcasted_iota(jnp.int32, (length, length), 0)
    col_index = lax.broadcasted_iota(jnp.int32, (length, length), 1)
    lower_mask = row_index >= col_index
    strict = row_index > col_index
    differ = cumulative[..., :, None] - cumulative[..., None, :]
    weights = jnp.where(lower_mask, jnp.exp(jnp.where(lower_mask, differ, 0.0)), 0.0)
    key_dots = jnp.einsum('...cd,...ed->...ce', keys_in, keys_in, precision=HIGH_PRECISION)
    system = jnp.where(strict, key_dots * weights * beta_gate[..., :, None], 0.0) + jnp.eye(length, dtype=jnp.float32)
    growth = jnp.exp(cumulative)
    right_side = jnp.concatenate([beta_gate[..., None] * values_in, (beta_gate * growth)[..., None] * keys_in], axis=-1)
    solved = jax.scipy.linalg.solve_triangular(system, right_side, lower=True, unit_diagonal=True)
    head_width = values_in.shape[-1]
    update_part = solved[..., :head_width]
    write_part = solved[..., head_width:]
    attend = jnp.einsum('...cd,...ed->...ce', queries, keys_in, precision=HIGH_PRECISION) * weights
    final_sum = cumulative[..., -1]
    carried_keys = jnp.exp(final_sum[..., None] - cumulative)[..., None] * keys_in
    return (update_part, write_part, attend, growth[..., None] * queries, carried_keys, jnp.exp(final_sum))

def block_output(update_part, write_part, attend, grown_query, current_state):
    incoming_value_rows = update_part - jnp.einsum('...ck,...kv->...cv', write_part, current_state, precision=HIGH_PRECISION)
    result = jnp.einsum('...ck,...kv->...cv', grown_query, current_state, precision=HIGH_PRECISION)
    result = result + jnp.einsum('...ce,...ev->...cv', attend, incoming_value_rows, precision=HIGH_PRECISION)
    return (result, incoming_value_rows)

def advance(current_state, incoming_value_rows, carried_keys, decay_total):
    return decay_total[..., None, None] * current_state + jnp.einsum('...ck,...cv->...kv', carried_keys, incoming_value_rows, precision=HIGH_PRECISION)

def reference(qkv_blocks, block_scales, gate_logits, conv_weight, decay_log, dt_bias, norm_gain):
    block_count = SEQUENCE_TOKENS // BLOCK
    coded = qkv_blocks.reshape(block_count, BLOCK, HK, 4 * HD)
    scale_rows = block_scales.reshape(block_count, BLOCK // QB, HK, 4)
    gate_rows = gate_logits.reshape(block_count, BLOCK, HK, 4)

    def advance_block(carried, inputs):
        current_state, previous = carried
        coded_now, scale_now, gate_now = inputs
        values = dequantize(coded_now, scale_now)
        extended = jnp.concatenate([previous, values], axis=0)
        mixed = convolve(extended, conv_weight, BLOCK)
        queries, keys_in, values_in, beta_gate, log_decay = split_heads(mixed, gate_now, decay_log, dt_bias)
        update_part, write_part, attend, grown_query, carried_keys, decay_total = block_terms(queries, keys_in, values_in, beta_gate, log_decay)
        outputs, incoming_value_rows = block_output(update_part, write_part, attend, grown_query, current_state)
        state_next = advance(current_state, incoming_value_rows, carried_keys, decay_total)
        scaled = outputs * lax.rsqrt(lax.optimization_barrier(jnp.mean(outputs * outputs, axis=-1, keepdims=True)) + EPS_NORM) * norm_gain
        return ((state_next, extended[BLOCK:]), jnp.swapaxes(scaled.astype(jnp.bfloat16), 0, 1))
    start_state = jnp.zeros((VALUE_HEADS, HD, HD), jnp.float32)
    start_rim = jnp.zeros((CONV - 1, HK, 4 * HD), jnp.float32)
    unused_carry, pieces = lax.scan(advance_block, (start_state, start_rim), (coded, scale_rows, gate_rows))
    return pieces.reshape(SEQUENCE_TOKENS, VALUE_HEADS, HD)
```

```python
import jax
import jax.numpy as jnp
from jax import lax
from jax.sharding import PartitionSpec as P

HD = 128
BLOCK = 128
QB = 32
CONV = 4


HIGH_PRECISION = lax.Precision.HIGHEST
EPS_NORM = 1e-06


def from_behind(value, axis, steps):
    count = lax.axis_size(axis)
    leading, last = (max(0, -steps), min(count, count - steps))
    return lax.ppermute(value, axis, [(source, source + steps) for source in range(leading, last)])


def dequantize(blocks, scales):
    token_count = blocks.shape[0]
    head_count = blocks.shape[1]
    quarter = blocks.shape[2] // 4
    shaped = blocks.astype(jnp.float32).reshape(token_count // QB, QB, head_count, 4, quarter)
    scaled = shaped * scales.astype(jnp.float32)[:, None, :, :, None]
    return scaled.reshape(token_count, head_count, 4 * quarter)


def convolve(extended, conv_weight, token_count):
    summed = conv_weight[0] * extended[0:token_count]
    for offset in range(1, CONV):
        summed = summed + conv_weight[offset] * extended[offset : offset + token_count]
    return jax.nn.silu(summed)


def unit_rows(matrix):
    return matrix * lax.rsqrt(jnp.sum(matrix * matrix, axis=-1, keepdims=True) + EPS_NORM)


def split_heads(mixed, gate_share, decay_log, dt_bias):
    token_count = mixed.shape[0]
    value_heads = 2 * mixed.shape[1]
    block_count = token_count // BLOCK
    queries = jnp.repeat(unit_rows(mixed[:, :, :HD]), 2, axis=1)
    keys_in = jnp.repeat(unit_rows(mixed[:, :, HD : 2 * HD]), 2, axis=1)
    values_in = mixed[:, :, 2 * HD :].reshape(token_count, value_heads, HD)
    gate_values = gate_share.astype(jnp.float32)
    beta_gate = jax.nn.sigmoid(gate_values[:, :, :2].reshape(token_count, value_heads))
    raw_decay = gate_values[:, :, 2:].reshape(token_count, value_heads)
    log_decay = -jnp.exp(decay_log) * jax.nn.softplus(raw_decay + dt_bias)

    def blocked(tensor):
        return jnp.swapaxes(tensor.reshape((block_count, BLOCK) + tensor.shape[1:]), 1, 2)

    return (
        blocked(queries),
        blocked(keys_in),
        blocked(values_in),
        blocked(beta_gate),
        blocked(log_decay),
    )


def lower_inverse(strict_part, length):
    negated = -strict_part
    eye_block = jnp.eye(length, dtype=jnp.float32)
    inverse = eye_block + negated
    power = negated
    for unused_level in range((length - 1).bit_length() - 1):
        power = jnp.einsum("...ij,...jk->...ik", power, power, precision=HIGH_PRECISION)
        inverse = inverse + jnp.einsum(
            "...ij,...jk->...ik", inverse, power, precision=HIGH_PRECISION
        )
    return inverse


def block_terms(queries, keys_in, values_in, beta_gate, log_decay):
    cumulative = jnp.cumsum(log_decay, axis=-1)
    length = log_decay.shape[-1]
    row_index = lax.broadcasted_iota(jnp.int32, (length, length), 0)
    col_index = lax.broadcasted_iota(jnp.int32, (length, length), 1)
    lower_mask = row_index >= col_index
    strict = row_index > col_index
    differ = cumulative[..., :, None] - cumulative[..., None, :]
    weights = jnp.where(lower_mask, jnp.exp(jnp.where(lower_mask, differ, 0.0)), 0.0)
    key_dots = jnp.einsum("...cd,...ed->...ce", keys_in, keys_in, precision=HIGH_PRECISION)
    strict_part = jnp.where(strict, key_dots * weights * beta_gate[..., :, None], 0.0)
    growth = jnp.exp(cumulative)
    right_side = jnp.concatenate(
        [beta_gate[..., None] * values_in, (beta_gate * growth)[..., None] * keys_in], axis=-1
    )
    inverse = lower_inverse(strict_part, length)
    solved = jnp.einsum("...ce,...ed->...cd", inverse, right_side, precision=HIGH_PRECISION)
    head_width = values_in.shape[-1]
    update_part = solved[..., :head_width]
    write_part = solved[..., head_width:]
    attend = jnp.einsum("...cd,...ed->...ce", queries, keys_in, precision=HIGH_PRECISION) * weights
    final_sum = cumulative[..., -1]
    carried_keys = jnp.exp(final_sum[..., None] - cumulative)[..., None] * keys_in
    return (
        update_part,
        write_part,
        attend,
        growth[..., None] * queries,
        carried_keys,
        jnp.exp(final_sum),
    )


def advance(current_state, incoming_value_rows, carried_keys, decay_total):
    return decay_total[..., None, None] * current_state + jnp.einsum(
        "...ck,...cv->...kv", carried_keys, incoming_value_rows, precision=HIGH_PRECISION
    )


def pair_update(passed_block_state, inputs):
    current_update, current_write, carried_now, decay_now = inputs
    target_values = jnp.concatenate([current_update, jnp.zeros_like(current_update)], axis=-1)
    incoming_value_rows = target_values - jnp.einsum(
        "zsg,zgj->zsj", current_write, passed_block_state, precision=HIGH_PRECISION
    )
    return advance(passed_block_state, incoming_value_rows, carried_now, decay_now)


def shifted(value, axis, steps):
    count = lax.axis_size(axis)
    return lax.ppermute(value, axis, [(source, source + steps) for source in range(count - steps)])


def incoming_state(pair, axis):
    count = lax.axis_size(axis)
    place = lax.axis_index(axis)
    state = pair[..., :HD]
    if count == 1:
        return jnp.zeros_like(state)
    width = 1
    while 2 * width < count:
        got = shifted(pair, axis, width)
        joined = jnp.einsum("hij,hjk->hik", pair[..., HD:], got, precision=HIGH_PRECISION)
        joined = joined + jnp.concatenate([pair[..., :HD], jnp.zeros_like(state)], axis=-1)
        pair = jnp.where(place >= width, joined, pair)
        width *= 2
    previous = shifted(pair, axis, 1)
    result = previous[..., :HD]
    if width + 1 < count:
        far_state = shifted(pair[..., :HD], axis, width + 1)
        result = result + jnp.einsum(
            "hij,hjk->hik", previous[..., HD:], far_state, precision=HIGH_PRECISION
        )
    return result


def step_pair(pair, inputs):
    return (pair_update(pair, inputs), pair)


def local(qkv_blocks, block_scales, gate_logits, conv_weight, decay_log, dt_bias, norm_gain):
    coded_share, scale_share, gate_share = (
        lax.all_to_all(qkv_blocks, "inner", split_axis=1, concat_axis=0, tiled=True),
        lax.all_to_all(block_scales, "inner", split_axis=1, concat_axis=0, tiled=True),
        lax.all_to_all(gate_logits, "inner", split_axis=1, concat_axis=0, tiled=True),
    )
    regrouped = dequantize(coded_share, scale_share)
    token_count = regrouped.shape[0]
    previous = from_behind(regrouped[token_count - CONV + 1 :], "outer", 1)
    mixed = convolve(jnp.concatenate([previous, regrouped], axis=0), conv_weight, token_count)
    queries, keys_in, values_in, beta_gate, log_decay = split_heads(
        mixed, gate_share, decay_log, dt_bias
    )
    update_part, write_part, attend, grown_query, carried_keys, decay_total = block_terms(
        queries, keys_in, values_in, beta_gate, log_decay
    )
    head_count = queries.shape[1]
    zero_state = jnp.zeros((head_count, HD, HD), jnp.float32)
    identity = jnp.broadcast_to(jnp.eye(HD, dtype=jnp.float32), (head_count, HD, HD))
    start_pair = jnp.concatenate([zero_state, identity], axis=-1)
    sequence = (update_part, write_part, carried_keys, decay_total)
    final_pair, start_pairs = lax.scan(step_pair, start_pair, sequence)
    incoming = incoming_state(final_pair, "outer")
    effective_query = grown_query - jnp.einsum(
        "...ce,...ek->...ck", attend, write_part, precision=HIGH_PRECISION
    )
    local_part = jnp.einsum(
        "...ce,...ev->...cv", attend, update_part, precision=HIGH_PRECISION
    )
    through_state = jnp.einsum(
        "...ck,...kj->...cj", effective_query, start_pairs, precision=HIGH_PRECISION
    )
    local_part = local_part + through_state[..., :HD]
    outputs = local_part + jnp.einsum(
        "bhck,hkv->bhcv", through_state[..., HD:], incoming, precision=HIGH_PRECISION
    )
    scaled = (
        outputs
        * lax.rsqrt(jnp.mean(outputs * outputs, axis=-1, keepdims=True) + EPS_NORM)
        * norm_gain
    )
    normed = scaled.astype(jnp.bfloat16)
    by_token = jnp.swapaxes(normed, 1, 2).reshape(token_count, head_count, HD)
    return lax.all_to_all(by_token, "inner", split_axis=0, concat_axis=1, tiled=True)


def solution(mesh):
    placed = (
        P(("outer", "inner"), None, None),
        P(("outer", "inner"), None, None),
        P(("outer", "inner"), None, None),
        P(None, "inner", None),
        P("inner"),
        P("inner"),
        P(),
    )
    return jax.shard_map(
        local,
        mesh=mesh,
        in_specs=placed,
        out_specs=P(("outer", "inner"), None, None),
        check_vma=False,
    )
```

```python
import jax
import jax.numpy as jnp
from jax import lax
from jax.sharding import PartitionSpec as P

HD = 128
BLOCK = 128
QB = 32
CONV = 4


HIGH_PRECISION = lax.Precision.HIGHEST
EPS_NORM = 1e-06


def convolve(extended, conv_weight, token_count):
    summed = conv_weight[0] * extended[0:token_count]
    for offset in range(1, CONV):
        summed = summed + conv_weight[offset] * extended[offset : offset + token_count]
    return jax.nn.silu(summed)


def unit_rows(matrix):
    return matrix * lax.rsqrt(jnp.sum(matrix * matrix, axis=-1, keepdims=True) + EPS_NORM)


def split_heads(mixed, gate_share, decay_log, dt_bias):
    token_count = mixed.shape[0]
    value_heads = 2 * mixed.shape[1]
    block_count = token_count // BLOCK
    query_heads = unit_rows(mixed[:, :, :HD])
    key_heads = unit_rows(mixed[:, :, HD : 2 * HD])
    queries = jnp.repeat(query_heads, 2, axis=1)
    keys_in = jnp.repeat(key_heads, 2, axis=1)
    values_in = mixed[:, :, 2 * HD :].reshape(token_count, value_heads, HD)
    gate_values = gate_share.astype(jnp.float32)
    beta_gate = jax.nn.sigmoid(gate_values[:, :, :2].reshape(token_count, value_heads))
    raw_decay = gate_values[:, :, 2:].reshape(token_count, value_heads)
    log_decay = -jnp.exp(decay_log) * jax.nn.softplus(raw_decay + dt_bias)

    def blocked(tensor):
        return jnp.swapaxes(tensor.reshape((block_count, BLOCK) + tensor.shape[1:]), 1, 2)

    return (
        blocked(query_heads),
        blocked(key_heads),
        blocked(queries),
        blocked(keys_in),
        blocked(values_in),
        blocked(beta_gate),
        blocked(log_decay),
    )


def lower_inverse(strict_part, length):
    negated = -strict_part
    eye_block = jnp.eye(length, dtype=jnp.float32)

    def level(unused_level, carried):
        inverse, power = carried
        power = jnp.einsum("...ij,...jk->...ik", power, power, precision=HIGH_PRECISION)
        inverse = inverse + jnp.einsum(
            "...ij,...jk->...ik", inverse, power, precision=HIGH_PRECISION
        )
        return (inverse, power)

    levels = (length - 1).bit_length() - 1
    return lax.fori_loop(0, levels, level, (eye_block + negated, negated))[0]


def block_terms(query_heads, key_heads, queries, keys_in, values_in, beta_gate, log_decay):
    cumulative = jnp.cumsum(log_decay, axis=-1)
    length = log_decay.shape[-1]
    row_index = lax.broadcasted_iota(jnp.int32, (length, length), 0)
    col_index = lax.broadcasted_iota(jnp.int32, (length, length), 1)
    lower_mask = row_index >= col_index
    strict = row_index > col_index
    differ = cumulative[..., :, None] - cumulative[..., None, :]
    weights = jnp.where(lower_mask, jnp.exp(jnp.where(lower_mask, differ, 0.0)), 0.0)
    both = jnp.concatenate([key_heads, query_heads], axis=-2)
    dots = jnp.einsum("...cd,...ed->...ce", both, key_heads, precision=HIGH_PRECISION)
    dots = jnp.repeat(dots, 2, axis=-3)
    key_dots = dots[..., :length, :]
    strict_part = jnp.where(strict, key_dots * weights * beta_gate[..., :, None], 0.0)
    growth = jnp.exp(cumulative)
    right_side = jnp.concatenate(
        [beta_gate[..., None] * values_in, (beta_gate * growth)[..., None] * keys_in], axis=-1
    )
    inverse = lower_inverse(strict_part, length)
    solved = jnp.einsum("...ce,...ed->...cd", inverse, right_side, precision=HIGH_PRECISION)
    attend = dots[..., length:, :] * weights
    final_sum = cumulative[..., -1]
    carried_keys = jnp.exp(final_sum[..., None] - cumulative)[..., None] * keys_in
    return (
        solved,
        attend,
        growth[..., None] * queries,
        carried_keys,
        jnp.exp(final_sum),
    )


def advance(current_state, incoming_value_rows, carried_keys, decay_total):
    return decay_total[..., None, None] * current_state + jnp.einsum(
        "...ck,...cv->...kv", carried_keys, incoming_value_rows, precision=HIGH_PRECISION
    )


def pair_update(passed_block_state, inputs):
    current_update, current_write, carried_now, decay_now = inputs
    target_values = jnp.concatenate([current_update, jnp.zeros_like(current_update)], axis=-1)
    incoming_value_rows = target_values - jnp.einsum(
        "zsg,zgj->zsj", current_write, passed_block_state, precision=HIGH_PRECISION
    )
    return advance(passed_block_state, incoming_value_rows, carried_now, decay_now)


def shifted(value, axis, steps):
    count = lax.axis_size(axis)
    return lax.ppermute(value, axis, [(source, source + steps) for source in range(count - steps)])


def incoming_state(pair, axis):
    count = lax.axis_size(axis)
    place = lax.axis_index(axis)
    state = pair[..., :HD]
    if count == 1:
        return jnp.zeros_like(state)
    width = 1
    while 2 * width < count:
        got = shifted(pair, axis, width)
        joined = jnp.einsum("hij,hjk->hik", pair[..., HD:], got, precision=HIGH_PRECISION)
        joined = joined + jnp.concatenate([pair[..., :HD], jnp.zeros_like(state)], axis=-1)
        pair = jnp.where(place >= width, joined, pair)
        width *= 2
    previous = shifted(pair, axis, 1)
    result = previous[..., :HD]
    if width + 1 < count:
        far_state = shifted(pair[..., :HD], axis, width + 1)
        result = result + jnp.einsum(
            "hij,hjk->hik", previous[..., HD:], far_state, precision=HIGH_PRECISION
        )
    return result


def step_pair(pair, inputs):
    return (pair_update(pair, inputs), pair)


def rim_from_behind(qkv_blocks, block_scales, head_share):
    outer_count = lax.axis_size("outer")
    inner_count = lax.axis_size("inner")
    token_count = qkv_blocks.shape[0]
    head_count = qkv_blocks.shape[1]
    quarter = qkv_blocks.shape[2] // 4
    tail = qkv_blocks[token_count - CONV + 1 :].astype(jnp.float32)
    tail = tail.reshape(CONV - 1, head_count, 4, quarter) * block_scales[-1].astype(
        jnp.float32
    )[None, :, :, None]
    tail = tail.reshape(CONV - 1, head_count, 4 * quarter)
    received = None
    for target in range(inner_count):
        piece = tail[:, target * head_share : (target + 1) * head_share]
        pairs = [
            ((block - 1) * inner_count + inner_count - 1, block * inner_count + target)
            for block in range(1, outer_count)
        ]
        got = lax.ppermute(piece, ("outer", "inner"), pairs)
        received = got if received is None else received + got
    return received


def local(qkv_blocks, block_scales, gate_logits, conv_weight, decay_log, dt_bias, norm_gain):
    inner_count = lax.axis_size("inner")
    own_tokens, head_count, channels = qkv_blocks.shape
    head_share = head_count // inner_count
    previous = rim_from_behind(qkv_blocks, block_scales, head_share)
    scale_rows = jnp.repeat(block_scales, QB, axis=0)
    extra = jnp.concatenate([scale_rows, gate_logits], axis=-1)
    extra_width = extra.shape[-1]
    extra_rows = own_tokens * extra_width // channels
    extra = jnp.swapaxes(extra, 0, 1).reshape(head_count, extra_rows, channels)
    packed = jnp.concatenate([qkv_blocks, jnp.swapaxes(extra, 0, 1)], axis=0)
    shared = lax.all_to_all(packed, "inner", split_axis=1, concat_axis=0, tiled=True)
    shared = shared.reshape(inner_count, own_tokens + extra_rows, head_share, channels)
    coded_share = shared[:, :own_tokens].reshape(inner_count * own_tokens, head_share, channels)
    extra_share = jnp.swapaxes(shared[:, own_tokens:], 1, 2).reshape(
        inner_count, head_share, own_tokens, extra_width
    )
    extra_share = jnp.swapaxes(extra_share, 1, 2).reshape(
        inner_count * own_tokens, head_share, extra_width
    )
    scale_share = extra_share[..., :4]
    gate_share = extra_share[..., 4:]
    token_count = coded_share.shape[0]
    quarter = channels // 4
    regrouped = (
        coded_share.astype(jnp.float32).reshape(token_count, head_share, 4, quarter)
        * scale_share.astype(jnp.float32)[..., None]
    ).reshape(token_count, head_share, channels)
    mixed = convolve(jnp.concatenate([previous, regrouped], axis=0), conv_weight, token_count)
    query_heads, key_heads, queries, keys_in, values_in, beta_gate, log_decay = split_heads(
        mixed, gate_share, decay_log, dt_bias
    )
    solved, attend, grown_query, carried_keys, decay_total = block_terms(
        query_heads, key_heads, queries, keys_in, values_in, beta_gate, log_decay
    )
    update_part = solved[..., :HD]
    write_part = solved[..., HD:]
    value_heads = queries.shape[1]
    zero_state = jnp.zeros((value_heads, HD, HD), jnp.float32)
    identity = jnp.broadcast_to(jnp.eye(HD, dtype=jnp.float32), (value_heads, HD, HD))
    start_pair = jnp.concatenate([zero_state, identity], axis=-1)
    sequence = (update_part, write_part, carried_keys, decay_total)
    final_pair, start_pairs = lax.scan(step_pair, start_pair, sequence)
    incoming = incoming_state(final_pair, "outer")
    attended = jnp.einsum("...ce,...ed->...cd", attend, solved, precision=HIGH_PRECISION)
    effective_query = grown_query - attended[..., HD:]
    through_state = jnp.einsum(
        "...ck,...kj->...cj", effective_query, start_pairs, precision=HIGH_PRECISION
    )
    local_part = attended[..., :HD] + through_state[..., :HD]
    outputs = local_part + jnp.einsum(
        "bhck,hkv->bhcv", through_state[..., HD:], incoming, precision=HIGH_PRECISION
    )
    scaled = (
        outputs
        * lax.rsqrt(jnp.mean(outputs * outputs, axis=-1, keepdims=True) + EPS_NORM)
        * norm_gain
    )
    normed = scaled.astype(jnp.bfloat16)
    by_token = jnp.swapaxes(normed, 1, 2).reshape(token_count, value_heads, HD)
    return lax.all_to_all(by_token, "inner", split_axis=0, concat_axis=1, tiled=True)


def solution(mesh):
    placed = (
        P(("outer", "inner"), None, None),
        P(("outer", "inner"), None, None),
        P(("outer", "inner"), None, None),
        P(None, "inner", None),
        P("inner"),
        P("inner"),
        P(),
    )
    return jax.shard_map(
        local,
        mesh=mesh,
        in_specs=placed,
        out_specs=P(("outer", "inner"), None, None),
        check_vma=False,
    )
```

```python
import jax
import jax.numpy as jnp
from jax import lax
from jax.sharding import PartitionSpec as P

HD = 128
BLOCK = 128
QB = 32
CONV = 4


HIGH_PRECISION = lax.Precision.HIGHEST
EPS_NORM = 1e-06


def convolve(extended, conv_weight, token_count):
    summed = conv_weight[0] * extended[0:token_count]
    for offset in range(1, CONV):
        summed = summed + conv_weight[offset] * extended[offset : offset + token_count]
    return jax.nn.silu(summed)


def unit_rows(matrix):
    return matrix * lax.rsqrt(jnp.sum(matrix * matrix, axis=-1, keepdims=True) + EPS_NORM)


def split_heads(mixed, gate_share, decay_log, dt_bias):
    token_count = mixed.shape[0]
    value_heads = 2 * mixed.shape[1]
    block_count = token_count // BLOCK
    query_heads = unit_rows(mixed[:, :, :HD])
    key_heads = unit_rows(mixed[:, :, HD : 2 * HD])
    queries = jnp.repeat(query_heads, 2, axis=1)
    keys_in = jnp.repeat(key_heads, 2, axis=1)
    values_in = mixed[:, :, 2 * HD :].reshape(token_count, value_heads, HD)
    gate_values = gate_share.astype(jnp.float32)
    beta_gate = jax.nn.sigmoid(gate_values[:, :, :2].reshape(token_count, value_heads))
    raw_decay = gate_values[:, :, 2:].reshape(token_count, value_heads)
    log_decay = -jnp.exp(decay_log) * jax.nn.softplus(raw_decay + dt_bias)

    def blocked(tensor):
        return jnp.swapaxes(tensor.reshape((block_count, BLOCK) + tensor.shape[1:]), 1, 2)

    return (
        blocked(query_heads),
        blocked(key_heads),
        blocked(queries),
        blocked(keys_in),
        blocked(values_in),
        blocked(beta_gate),
        blocked(log_decay),
    )


def lower_inverse(strict_part, length):
    negated = -strict_part
    eye_block = jnp.eye(length, dtype=jnp.float32)
    inverse = eye_block + negated
    power = negated
    for unused_level in range((length - 1).bit_length() - 1):
        power = jnp.einsum("...ij,...jk->...ik", power, power, precision=HIGH_PRECISION)
        inverse = inverse + jnp.einsum(
            "...ij,...jk->...ik", inverse, power, precision=HIGH_PRECISION
        )
    return inverse


def block_terms(query_heads, key_heads, queries, keys_in, values_in, beta_gate, log_decay):
    cumulative = jnp.cumsum(log_decay, axis=-1)
    length = log_decay.shape[-1]
    row_index = lax.broadcasted_iota(jnp.int32, (length, length), 0)
    col_index = lax.broadcasted_iota(jnp.int32, (length, length), 1)
    lower_mask = row_index >= col_index
    strict = row_index > col_index
    differ = cumulative[..., :, None] - cumulative[..., None, :]
    weights = jnp.where(lower_mask, jnp.exp(jnp.where(lower_mask, differ, 0.0)), 0.0)
    both = jnp.concatenate([key_heads, query_heads], axis=-2)
    dots = jnp.einsum("...cd,...ed->...ce", both, key_heads, precision=HIGH_PRECISION)
    dots = jnp.repeat(dots, 2, axis=-3)
    key_dots = dots[..., :length, :]
    strict_part = jnp.where(strict, key_dots * weights * beta_gate[..., :, None], 0.0)
    growth = jnp.exp(cumulative)
    right_side = jnp.concatenate(
        [beta_gate[..., None] * values_in, (beta_gate * growth)[..., None] * keys_in], axis=-1
    )
    inverse = lower_inverse(strict_part, length)
    solved = jnp.einsum("...ce,...ed->...cd", inverse, right_side, precision=HIGH_PRECISION)
    attend = dots[..., length:, :] * weights
    final_sum = cumulative[..., -1]
    carried_keys = jnp.exp(final_sum[..., None] - cumulative)[..., None] * keys_in
    return (
        solved,
        attend,
        growth[..., None] * queries,
        carried_keys,
        jnp.exp(final_sum),
    )


def advance(current_state, incoming_value_rows, carried_keys, decay_total):
    return decay_total[..., None, None] * current_state + jnp.einsum(
        "...ck,...cv->...kv", carried_keys, incoming_value_rows, precision=HIGH_PRECISION
    )


def pair_update(passed_block_state, inputs):
    current_update, current_write, carried_now, decay_now = inputs
    target_values = jnp.concatenate([current_update, jnp.zeros_like(current_update)], axis=-1)
    incoming_value_rows = target_values - jnp.einsum(
        "zsg,zgj->zsj", current_write, passed_block_state, precision=HIGH_PRECISION
    )
    return advance(passed_block_state, incoming_value_rows, carried_now, decay_now)


def shifted(value, axis, steps):
    count = lax.axis_size(axis)
    return lax.ppermute(value, axis, [(source, source + steps) for source in range(count - steps)])


def incoming_state(pair, axis):
    count = lax.axis_size(axis)
    place = lax.axis_index(axis)
    state = pair[..., :HD]
    if count == 1:
        return jnp.zeros_like(state)
    width = 1
    while 2 * width < count:
        got = shifted(pair, axis, width)
        joined = jnp.einsum("hij,hjk->hik", pair[..., HD:], got, precision=HIGH_PRECISION)
        joined = joined + jnp.concatenate([pair[..., :HD], jnp.zeros_like(state)], axis=-1)
        pair = jnp.where(place >= width, joined, pair)
        width *= 2
    previous = shifted(pair, axis, 1)
    result = previous[..., :HD]
    if width + 1 < count:
        far_state = shifted(pair[..., :HD], axis, width + 1)
        result = result + jnp.einsum(
            "hij,hjk->hik", previous[..., HD:], far_state, precision=HIGH_PRECISION
        )
    return result


def step_pair(pair, inputs):
    return (pair_update(pair, inputs), pair)


def rim_from_behind(qkv_blocks, block_scales, head_share):
    outer_count = lax.axis_size("outer")
    inner_count = lax.axis_size("inner")
    token_count = qkv_blocks.shape[0]
    head_count = qkv_blocks.shape[1]
    quarter = qkv_blocks.shape[2] // 4
    tail = qkv_blocks[token_count - CONV + 1 :].astype(jnp.float32)
    tail = tail.reshape(CONV - 1, head_count, 4, quarter) * block_scales[-1].astype(
        jnp.float32
    )[None, :, :, None]
    tail = tail.reshape(CONV - 1, head_count, 4 * quarter)
    received = None
    for target in range(inner_count):
        piece = tail[:, target * head_share : (target + 1) * head_share]
        pairs = [
            ((block - 1) * inner_count + inner_count - 1, block * inner_count + target)
            for block in range(1, outer_count)
        ]
        got = lax.ppermute(piece, ("outer", "inner"), pairs)
        received = got if received is None else received + got
    return received


def local(qkv_blocks, block_scales, gate_logits, conv_weight, decay_log, dt_bias, norm_gain):
    inner_count = lax.axis_size("inner")
    own_tokens, head_count, channels = qkv_blocks.shape
    head_share = head_count // inner_count
    previous = rim_from_behind(qkv_blocks, block_scales, head_share)
    scale_rows = jnp.repeat(block_scales, QB, axis=0)
    extra = jnp.concatenate([scale_rows, gate_logits], axis=-1)
    extra_width = extra.shape[-1]
    extra_rows = own_tokens * extra_width // channels
    extra = jnp.swapaxes(extra, 0, 1).reshape(head_count, extra_rows, channels)
    packed = jnp.concatenate([qkv_blocks, jnp.swapaxes(extra, 0, 1)], axis=0)
    shared = lax.all_to_all(packed, "inner", split_axis=1, concat_axis=0, tiled=True)
    shared = shared.reshape(inner_count, own_tokens + extra_rows, head_share, channels)
    coded_share = shared[:, :own_tokens].reshape(inner_count * own_tokens, head_share, channels)
    extra_share = jnp.swapaxes(shared[:, own_tokens:], 1, 2).reshape(
        inner_count, head_share, own_tokens, extra_width
    )
    extra_share = jnp.swapaxes(extra_share, 1, 2).reshape(
        inner_count * own_tokens, head_share, extra_width
    )
    scale_share = extra_share[..., :4]
    gate_share = extra_share[..., 4:]
    token_count = coded_share.shape[0]
    quarter = channels // 4
    regrouped = (
        coded_share.astype(jnp.float32).reshape(token_count, head_share, 4, quarter)
        * scale_share.astype(jnp.float32)[..., None]
    ).reshape(token_count, head_share, channels)
    mixed = convolve(jnp.concatenate([previous, regrouped], axis=0), conv_weight, token_count)
    query_heads, key_heads, queries, keys_in, values_in, beta_gate, log_decay = split_heads(
        mixed, gate_share, decay_log, dt_bias
    )
    solved, attend, grown_query, carried_keys, decay_total = block_terms(
        query_heads, key_heads, queries, keys_in, values_in, beta_gate, log_decay
    )
    update_part = solved[..., :HD]
    write_part = solved[..., HD:]
    value_heads = queries.shape[1]
    zero_state = jnp.zeros((value_heads, HD, HD), jnp.float32)
    identity = jnp.broadcast_to(jnp.eye(HD, dtype=jnp.float32), (value_heads, HD, HD))
    start_pair = jnp.concatenate([zero_state, identity], axis=-1)
    sequence = (update_part, write_part, carried_keys, decay_total)
    final_pair, start_pairs = lax.scan(step_pair, start_pair, sequence)
    incoming = incoming_state(final_pair, "outer")
    attended = jnp.einsum("...ce,...ed->...cd", attend, solved, precision=HIGH_PRECISION)
    effective_query = grown_query - attended[..., HD:]
    through_state = jnp.einsum(
        "...ck,...kj->...cj", effective_query, start_pairs, precision=HIGH_PRECISION
    )
    local_part = attended[..., :HD] + through_state[..., :HD]
    outputs = local_part + jnp.einsum(
        "bhck,hkv->bhcv", through_state[..., HD:], incoming, precision=HIGH_PRECISION
    )
    scaled = (
        outputs
        * lax.rsqrt(jnp.mean(outputs * outputs, axis=-1, keepdims=True) + EPS_NORM)
        * norm_gain
    )
    normed = scaled.astype(jnp.bfloat16)
    by_token = jnp.swapaxes(normed, 1, 2).reshape(token_count, value_heads, HD)
    return lax.all_to_all(by_token, "inner", split_axis=0, concat_axis=1, tiled=True)


def solution(mesh):
    placed = (
        P(("outer", "inner"), None, None),
        P(("outer", "inner"), None, None),
        P(("outer", "inner"), None, None),
        P(None, "inner", None),
        P("inner"),
        P("inner"),
        P(),
    )
    return jax.shard_map(
        local,
        mesh=mesh,
        in_specs=placed,
        out_specs=P(("outer", "inner"), None, None),
        check_vma=False,
    )
```

```python
import jax
import jax.numpy as jnp
from jax import lax
from jax.sharding import PartitionSpec as P

HD = 128
BLOCK = 128
QB = 32
CONV = 4


HIGH_PRECISION = lax.Precision.HIGHEST
EPS_NORM = 1e-06


def convolve(extended, conv_weight, token_count):
    summed = conv_weight[0] * extended[0:token_count]
    for offset in range(1, CONV):
        summed = summed + conv_weight[offset] * extended[offset : offset + token_count]
    return jax.nn.silu(summed)


def unit_rows(matrix):
    return matrix * lax.rsqrt(jnp.sum(matrix * matrix, axis=-1, keepdims=True) + EPS_NORM)


def split_heads(mixed, gate_share, decay_log, dt_bias):
    token_count = mixed.shape[0]
    value_heads = 2 * mixed.shape[1]
    block_count = token_count // BLOCK
    queries = jnp.repeat(unit_rows(mixed[:, :, :HD]), 2, axis=1)
    keys_in = jnp.repeat(unit_rows(mixed[:, :, HD : 2 * HD]), 2, axis=1)
    values_in = mixed[:, :, 2 * HD :].reshape(token_count, value_heads, HD)
    gate_values = gate_share.astype(jnp.float32)
    beta_gate = jax.nn.sigmoid(gate_values[:, :, :2].reshape(token_count, value_heads))
    raw_decay = gate_values[:, :, 2:].reshape(token_count, value_heads)
    log_decay = -jnp.exp(decay_log) * jax.nn.softplus(raw_decay + dt_bias)

    def blocked(tensor):
        return jnp.swapaxes(tensor.reshape((block_count, BLOCK) + tensor.shape[1:]), 1, 2)

    return (
        blocked(queries),
        blocked(keys_in),
        blocked(values_in),
        blocked(beta_gate),
        blocked(log_decay),
    )


def lower_inverse(strict_part, length):
    negated = -strict_part
    eye_block = jnp.eye(length, dtype=jnp.float32)
    inverse = eye_block + negated
    power = negated
    for unused_level in range((length - 1).bit_length() - 1):
        power = jnp.einsum("...ij,...jk->...ik", power, power, precision=HIGH_PRECISION)
        inverse = inverse + jnp.einsum(
            "...ij,...jk->...ik", inverse, power, precision=HIGH_PRECISION
        )
    return inverse


def block_terms(queries, keys_in, values_in, beta_gate, log_decay):
    cumulative = jnp.cumsum(log_decay, axis=-1)
    length = log_decay.shape[-1]
    row_index = lax.broadcasted_iota(jnp.int32, (length, length), 0)
    col_index = lax.broadcasted_iota(jnp.int32, (length, length), 1)
    lower_mask = row_index >= col_index
    strict = row_index > col_index
    differ = cumulative[..., :, None] - cumulative[..., None, :]
    weights = jnp.where(lower_mask, jnp.exp(jnp.where(lower_mask, differ, 0.0)), 0.0)
    key_dots = jnp.einsum("...cd,...ed->...ce", keys_in, keys_in, precision=HIGH_PRECISION)
    strict_part = jnp.where(strict, key_dots * weights * beta_gate[..., :, None], 0.0)
    growth = jnp.exp(cumulative)
    right_side = jnp.concatenate(
        [beta_gate[..., None] * values_in, (beta_gate * growth)[..., None] * keys_in], axis=-1
    )
    inverse = lower_inverse(strict_part, length)
    solved = jnp.einsum("...ce,...ed->...cd", inverse, right_side, precision=HIGH_PRECISION)
    head_width = values_in.shape[-1]
    update_part = solved[..., :head_width]
    write_part = solved[..., head_width:]
    attend = jnp.einsum("...cd,...ed->...ce", queries, keys_in, precision=HIGH_PRECISION) * weights
    final_sum = cumulative[..., -1]
    carried_keys = jnp.exp(final_sum[..., None] - cumulative)[..., None] * keys_in
    return (
        update_part,
        write_part,
        attend,
        growth[..., None] * queries,
        carried_keys,
        jnp.exp(final_sum),
    )


def advance(current_state, incoming_value_rows, carried_keys, decay_total):
    return decay_total[..., None, None] * current_state + jnp.einsum(
        "...ck,...cv->...kv", carried_keys, incoming_value_rows, precision=HIGH_PRECISION
    )


def pair_update(passed_block_state, inputs):
    current_update, current_write, carried_now, decay_now = inputs
    target_values = jnp.concatenate([current_update, jnp.zeros_like(current_update)], axis=-1)
    incoming_value_rows = target_values - jnp.einsum(
        "zsg,zgj->zsj", current_write, passed_block_state, precision=HIGH_PRECISION
    )
    return advance(passed_block_state, incoming_value_rows, carried_now, decay_now)


def shifted(value, axis, steps):
    count = lax.axis_size(axis)
    return lax.ppermute(value, axis, [(source, source + steps) for source in range(count - steps)])


def incoming_state(pair, axis):
    count = lax.axis_size(axis)
    place = lax.axis_index(axis)
    state = pair[..., :HD]
    if count == 1:
        return jnp.zeros_like(state)
    width = 1
    while 2 * width < count:
        got = shifted(pair, axis, width)
        joined = jnp.einsum("hij,hjk->hik", pair[..., HD:], got, precision=HIGH_PRECISION)
        joined = joined + jnp.concatenate([pair[..., :HD], jnp.zeros_like(state)], axis=-1)
        pair = jnp.where(place >= width, joined, pair)
        width *= 2
    previous = shifted(pair, axis, 1)
    result = previous[..., :HD]
    if width + 1 < count:
        far_state = shifted(pair[..., :HD], axis, width + 1)
        result = result + jnp.einsum(
            "hij,hjk->hik", previous[..., HD:], far_state, precision=HIGH_PRECISION
        )
    return result


def step_pair(pair, inputs):
    return (pair_update(pair, inputs), pair)


def rim_from_behind(qkv_blocks, block_scales, head_share):
    outer_count = lax.axis_size("outer")
    inner_count = lax.axis_size("inner")
    token_count = qkv_blocks.shape[0]
    head_count = qkv_blocks.shape[1]
    quarter = qkv_blocks.shape[2] // 4
    tail = qkv_blocks[token_count - CONV + 1 :].astype(jnp.float32)
    tail = tail.reshape(CONV - 1, head_count, 4, quarter) * block_scales[-1].astype(
        jnp.float32
    )[None, :, :, None]
    tail = tail.reshape(CONV - 1, head_count, 4 * quarter)
    received = None
    for target in range(inner_count):
        piece = tail[:, target * head_share : (target + 1) * head_share]
        pairs = [
            ((block - 1) * inner_count + inner_count - 1, block * inner_count + target)
            for block in range(1, outer_count)
        ]
        got = lax.ppermute(piece, ("outer", "inner"), pairs)
        received = got if received is None else received + got
    return received


def local(qkv_blocks, block_scales, gate_logits, conv_weight, decay_log, dt_bias, norm_gain):
    inner_count = lax.axis_size("inner")
    head_count, channels = qkv_blocks.shape[1], qkv_blocks.shape[2]
    head_share = head_count // inner_count
    previous = rim_from_behind(qkv_blocks, block_scales, head_share)
    side = jnp.concatenate([jnp.repeat(block_scales, QB, axis=0), gate_logits], axis=-1)
    coded_share = lax.all_to_all(qkv_blocks, "inner", split_axis=1, concat_axis=0, tiled=True)
    side_share = lax.all_to_all(side, "inner", split_axis=1, concat_axis=0, tiled=True)
    scale_share = side_share[..., :4]
    gate_share = side_share[..., 4:]
    token_count = coded_share.shape[0]
    quarter = channels // 4
    regrouped = (
        coded_share.astype(jnp.float32).reshape(token_count, head_share, 4, quarter)
        * scale_share.astype(jnp.float32)[..., None]
    ).reshape(token_count, head_share, channels)
    mixed = convolve(jnp.concatenate([previous, regrouped], axis=0), conv_weight, token_count)
    queries, keys_in, values_in, beta_gate, log_decay = split_heads(
        mixed, gate_share, decay_log, dt_bias
    )
    update_part, write_part, attend, grown_query, carried_keys, decay_total = block_terms(
        queries, keys_in, values_in, beta_gate, log_decay
    )
    head_count = queries.shape[1]
    zero_state = jnp.zeros((head_count, HD, HD), jnp.float32)
    identity = jnp.broadcast_to(jnp.eye(HD, dtype=jnp.float32), (head_count, HD, HD))
    start_pair = jnp.concatenate([zero_state, identity], axis=-1)
    sequence = (update_part, write_part, carried_keys, decay_total)
    final_pair, start_pairs = lax.scan(step_pair, start_pair, sequence)
    incoming = incoming_state(final_pair, "outer")
    effective_query = grown_query - jnp.einsum(
        "...ce,...ek->...ck", attend, write_part, precision=HIGH_PRECISION
    )
    local_part = jnp.einsum(
        "...ce,...ev->...cv", attend, update_part, precision=HIGH_PRECISION
    )
    through_state = jnp.einsum(
        "...ck,...kj->...cj", effective_query, start_pairs, precision=HIGH_PRECISION
    )
    local_part = local_part + through_state[..., :HD]
    outputs = local_part + jnp.einsum(
        "bhck,hkv->bhcv", through_state[..., HD:], incoming, precision=HIGH_PRECISION
    )
    scaled = (
        outputs
        * lax.rsqrt(jnp.mean(outputs * outputs, axis=-1, keepdims=True) + EPS_NORM)
        * norm_gain
    )
    normed = scaled.astype(jnp.bfloat16)
    by_token = jnp.swapaxes(normed, 1, 2).reshape(token_count, head_count, HD)
    return lax.all_to_all(by_token, "inner", split_axis=0, concat_axis=1, tiled=True)


def solution(mesh):
    placed = (
        P(("outer", "inner"), None, None),
        P(("outer", "inner"), None, None),
        P(("outer", "inner"), None, None),
        P(None, "inner", None),
        P("inner"),
        P("inner"),
        P(),
    )
    return jax.shard_map(
        local,
        mesh=mesh,
        in_specs=placed,
        out_specs=P(("outer", "inner"), None, None),
        check_vma=False,
    )
```

```python
import jax
import jax.numpy as jnp
from jax import lax
from jax.sharding import PartitionSpec as P

HD = 128
BLOCK = 128
QB = 32
CONV = 4


HIGH_PRECISION = lax.Precision.HIGHEST
EPS_NORM = 1e-06


def from_behind(value, axis, steps):
    count = lax.axis_size(axis)
    leading, last = (max(0, -steps), min(count, count - steps))
    return lax.ppermute(value, axis, [(source, source + steps) for source in range(leading, last)])


def dequantize(blocks, scales):
    token_count = blocks.shape[0]
    channels = blocks.shape[2]
    quarter = channels // 4
    per_token = jnp.repeat(scales.astype(jnp.float32), QB, axis=0)
    group = lax.broadcasted_iota(jnp.int32, (1, 1, channels), 2) // quarter
    spread = jnp.broadcast_to(per_token[..., 0:1], blocks.shape)
    for part in range(1, 4):
        spread = jnp.where(group == part, per_token[..., part : part + 1], spread)
    return blocks.astype(jnp.float32) * spread


def convolve(extended, conv_weight, token_count):
    summed = conv_weight[0] * extended[0:token_count]
    for offset in range(1, CONV):
        summed = summed + conv_weight[offset] * extended[offset : offset + token_count]
    return jax.nn.silu(summed)


def unit_rows(matrix):
    return matrix * lax.rsqrt(jnp.sum(matrix * matrix, axis=-1, keepdims=True) + EPS_NORM)


def split_heads(mixed, gate_share, decay_log, dt_bias):
    token_count = mixed.shape[0]
    value_heads = 2 * mixed.shape[1]
    block_count = token_count // BLOCK
    queries = jnp.repeat(unit_rows(mixed[:, :, :HD]), 2, axis=1)
    keys_in = jnp.repeat(unit_rows(mixed[:, :, HD : 2 * HD]), 2, axis=1)
    values_in = mixed[:, :, 2 * HD :].reshape(token_count, value_heads, HD)
    gate_values = gate_share.astype(jnp.float32)
    beta_gate = jax.nn.sigmoid(gate_values[:, :, :2].reshape(token_count, value_heads))
    raw_decay = gate_values[:, :, 2:].reshape(token_count, value_heads)
    log_decay = -jnp.exp(decay_log) * jax.nn.softplus(raw_decay + dt_bias)

    def blocked(tensor):
        return jnp.swapaxes(tensor.reshape((block_count, BLOCK) + tensor.shape[1:]), 1, 2)

    return (
        blocked(queries),
        blocked(keys_in),
        blocked(values_in),
        blocked(beta_gate),
        blocked(log_decay),
    )


def lower_inverse(strict_part, length):
    negated = -strict_part
    eye_block = jnp.eye(length, dtype=jnp.float32)
    inverse = eye_block + negated
    power = negated
    for unused_level in range((length - 1).bit_length() - 1):
        power = jnp.einsum("...ij,...jk->...ik", power, power, precision=HIGH_PRECISION)
        inverse = inverse + jnp.einsum(
            "...ij,...jk->...ik", inverse, power, precision=HIGH_PRECISION
        )
    return inverse


def block_terms(queries, keys_in, values_in, beta_gate, log_decay):
    cumulative = jnp.cumsum(log_decay, axis=-1)
    length = log_decay.shape[-1]
    row_index = lax.broadcasted_iota(jnp.int32, (length, length), 0)
    col_index = lax.broadcasted_iota(jnp.int32, (length, length), 1)
    lower_mask = row_index >= col_index
    strict = row_index > col_index
    differ = cumulative[..., :, None] - cumulative[..., None, :]
    weights = jnp.where(lower_mask, jnp.exp(jnp.where(lower_mask, differ, 0.0)), 0.0)
    key_dots = jnp.einsum("...cd,...ed->...ce", keys_in, keys_in, precision=HIGH_PRECISION)
    strict_part = jnp.where(strict, key_dots * weights * beta_gate[..., :, None], 0.0)
    growth = jnp.exp(cumulative)
    right_side = jnp.concatenate(
        [beta_gate[..., None] * values_in, (beta_gate * growth)[..., None] * keys_in], axis=-1
    )
    inverse = lower_inverse(strict_part, length)
    solved = jnp.einsum("...ce,...ed->...cd", inverse, right_side, precision=HIGH_PRECISION)
    head_width = values_in.shape[-1]
    update_part = solved[..., :head_width]
    write_part = solved[..., head_width:]
    attend = jnp.einsum("...cd,...ed->...ce", queries, keys_in, precision=HIGH_PRECISION) * weights
    final_sum = cumulative[..., -1]
    carried_keys = jnp.exp(final_sum[..., None] - cumulative)[..., None] * keys_in
    return (
        update_part,
        write_part,
        attend,
        growth[..., None] * queries,
        carried_keys,
        jnp.exp(final_sum),
    )


def advance(current_state, incoming_value_rows, carried_keys, decay_total):
    return decay_total[..., None, None] * current_state + jnp.einsum(
        "...ck,...cv->...kv", carried_keys, incoming_value_rows, precision=HIGH_PRECISION
    )


def pair_update(passed_block_state, inputs):
    current_update, current_write, carried_now, decay_now = inputs
    target_values = jnp.concatenate([current_update, jnp.zeros_like(current_update)], axis=-1)
    incoming_value_rows = target_values - jnp.einsum(
        "zsg,zgj->zsj", current_write, passed_block_state, precision=HIGH_PRECISION
    )
    return advance(passed_block_state, incoming_value_rows, carried_now, decay_now)


def shifted(value, axis, steps):
    count = lax.axis_size(axis)
    return lax.ppermute(value, axis, [(source, source + steps) for source in range(count - steps)])


def incoming_state(pair, axis):
    count = lax.axis_size(axis)
    place = lax.axis_index(axis)
    state = pair[..., :HD]
    if count == 1:
        return jnp.zeros_like(state)
    width = 1
    while 2 * width < count:
        got = shifted(pair, axis, width)
        joined = jnp.einsum("hij,hjk->hik", pair[..., HD:], got, precision=HIGH_PRECISION)
        joined = joined + jnp.concatenate([pair[..., :HD], jnp.zeros_like(state)], axis=-1)
        pair = jnp.where(place >= width, joined, pair)
        width *= 2
    previous = shifted(pair, axis, 1)
    result = previous[..., :HD]
    if width + 1 < count:
        far_state = shifted(pair[..., :HD], axis, width + 1)
        result = result + jnp.einsum(
            "hij,hjk->hik", previous[..., HD:], far_state, precision=HIGH_PRECISION
        )
    return result


def step_pair(pair, inputs):
    return (pair_update(pair, inputs), pair)


def local(qkv_blocks, block_scales, gate_logits, conv_weight, decay_log, dt_bias, norm_gain):
    coded_share, scale_share, gate_share = (
        lax.all_to_all(qkv_blocks, "inner", split_axis=1, concat_axis=0, tiled=True),
        lax.all_to_all(block_scales, "inner", split_axis=1, concat_axis=0, tiled=True),
        lax.all_to_all(gate_logits, "inner", split_axis=1, concat_axis=0, tiled=True),
    )
    regrouped = dequantize(coded_share, scale_share)
    token_count = regrouped.shape[0]
    previous = from_behind(regrouped[token_count - CONV + 1 :], "outer", 1)
    mixed = convolve(jnp.concatenate([previous, regrouped], axis=0), conv_weight, token_count)
    queries, keys_in, values_in, beta_gate, log_decay = split_heads(
        mixed, gate_share, decay_log, dt_bias
    )
    update_part, write_part, attend, grown_query, carried_keys, decay_total = block_terms(
        queries, keys_in, values_in, beta_gate, log_decay
    )
    head_count = queries.shape[1]
    zero_state = jnp.zeros((head_count, HD, HD), jnp.float32)
    identity = jnp.broadcast_to(jnp.eye(HD, dtype=jnp.float32), (head_count, HD, HD))
    start_pair = jnp.concatenate([zero_state, identity], axis=-1)
    sequence = (update_part, write_part, carried_keys, decay_total)
    final_pair, start_pairs = lax.scan(step_pair, start_pair, sequence)
    incoming = incoming_state(final_pair, "outer")
    effective_query = grown_query - jnp.einsum(
        "...ce,...ek->...ck", attend, write_part, precision=HIGH_PRECISION
    )
    local_part = jnp.einsum(
        "...ce,...ev->...cv", attend, update_part, precision=HIGH_PRECISION
    )
    through_state = jnp.einsum(
        "...ck,...kj->...cj", effective_query, start_pairs, precision=HIGH_PRECISION
    )
    local_part = local_part + through_state[..., :HD]
    outputs = local_part + jnp.einsum(
        "bhck,hkv->bhcv", through_state[..., HD:], incoming, precision=HIGH_PRECISION
    )
    scaled = (
        outputs
        * lax.rsqrt(jnp.mean(outputs * outputs, axis=-1, keepdims=True) + EPS_NORM)
        * norm_gain
    )
    normed = scaled.astype(jnp.bfloat16)
    by_token = jnp.swapaxes(normed, 1, 2).reshape(token_count, head_count, HD)
    return lax.all_to_all(by_token, "inner", split_axis=0, concat_axis=1, tiled=True)


def solution(mesh):
    placed = (
        P(("outer", "inner"), None, None),
        P(("outer", "inner"), None, None),
        P(("outer", "inner"), None, None),
        P(None, "inner", None),
        P("inner"),
        P("inner"),
        P(),
    )
    return jax.shard_map(
        local,
        mesh=mesh,
        in_specs=placed,
        out_specs=P(("outer", "inner"), None, None),
        check_vma=False,
    )
```

```python
import jax
import jax.numpy as jnp
from jax import lax
from jax.sharding import PartitionSpec as P

HD = 128
BLOCK = 128
QB = 32
CONV = 4


HIGH_PRECISION = lax.Precision.HIGHEST
EPS_NORM = 1e-06


def from_behind(value, axis, steps):
    count = lax.axis_size(axis)
    leading, last = (max(0, -steps), min(count, count - steps))
    return lax.ppermute(value, axis, [(source, source + steps) for source in range(leading, last)])


def dequantize(blocks, scales):
    token_count = blocks.shape[0]
    channels = blocks.shape[2]
    quarter = channels // 4
    per_token = jnp.repeat(scales.astype(jnp.float32), QB, axis=0)
    group = lax.broadcasted_iota(jnp.int32, (1, 1, channels), 2) // quarter
    spread = jnp.broadcast_to(per_token[..., 0:1], blocks.shape)
    for part in range(1, 4):
        spread = jnp.where(group == part, per_token[..., part : part + 1], spread)
    return blocks.astype(jnp.float32) * spread


def convolve(extended, conv_weight, token_count):
    summed = conv_weight[0] * extended[0:token_count]
    for offset in range(1, CONV):
        summed = summed + conv_weight[offset] * extended[offset : offset + token_count]
    return jax.nn.silu(summed)


def unit_rows(matrix):
    return matrix * lax.rsqrt(jnp.sum(matrix * matrix, axis=-1, keepdims=True) + EPS_NORM)


def split_heads(mixed, gate_share, decay_log, dt_bias):
    token_count = mixed.shape[0]
    value_heads = 2 * mixed.shape[1]
    block_count = token_count // BLOCK
    queries = jnp.repeat(unit_rows(mixed[:, :, :HD]), 2, axis=1)
    keys_in = jnp.repeat(unit_rows(mixed[:, :, HD : 2 * HD]), 2, axis=1)
    values_in = mixed[:, :, 2 * HD :].reshape(token_count, value_heads, HD)
    gate_values = gate_share.astype(jnp.float32)
    beta_gate = jax.nn.sigmoid(gate_values[:, :, :2].reshape(token_count, value_heads))
    raw_decay = gate_values[:, :, 2:].reshape(token_count, value_heads)
    log_decay = -jnp.exp(decay_log) * jax.nn.softplus(raw_decay + dt_bias)

    def blocked(tensor):
        return jnp.swapaxes(tensor.reshape((block_count, BLOCK) + tensor.shape[1:]), 1, 2)

    return (
        blocked(queries),
        blocked(keys_in),
        blocked(values_in),
        blocked(beta_gate),
        blocked(log_decay),
    )


def lower_inverse(strict_part, length):
    negated = -strict_part
    eye_block = jnp.eye(length, dtype=jnp.float32)
    inverse = eye_block + negated
    power = negated
    for unused_level in range((length - 1).bit_length() - 1):
        power = jnp.einsum("...ij,...jk->...ik", power, power, precision=HIGH_PRECISION)
        inverse = inverse + jnp.einsum(
            "...ij,...jk->...ik", inverse, power, precision=HIGH_PRECISION
        )
    return inverse


def block_terms(queries, keys_in, values_in, beta_gate, log_decay):
    cumulative = jnp.cumsum(log_decay, axis=-1)
    length = log_decay.shape[-1]
    row_index = lax.broadcasted_iota(jnp.int32, (length, length), 0)
    col_index = lax.broadcasted_iota(jnp.int32, (length, length), 1)
    lower_mask = row_index >= col_index
    strict = row_index > col_index
    differ = cumulative[..., :, None] - cumulative[..., None, :]
    weights = jnp.where(lower_mask, jnp.exp(jnp.where(lower_mask, differ, 0.0)), 0.0)
    key_dots = jnp.einsum("...cd,...ed->...ce", keys_in, keys_in, precision=HIGH_PRECISION)
    strict_part = jnp.where(strict, key_dots * weights * beta_gate[..., :, None], 0.0)
    growth = jnp.exp(cumulative)
    right_side = jnp.concatenate(
        [beta_gate[..., None] * values_in, (beta_gate * growth)[..., None] * keys_in], axis=-1
    )
    inverse = lower_inverse(strict_part, length)
    solved = jnp.einsum("...ce,...ed->...cd", inverse, right_side, precision=HIGH_PRECISION)
    head_width = values_in.shape[-1]
    update_part = solved[..., :head_width]
    write_part = solved[..., head_width:]
    attend = jnp.einsum("...cd,...ed->...ce", queries, keys_in, precision=HIGH_PRECISION) * weights
    final_sum = cumulative[..., -1]
    carried_keys = jnp.exp(final_sum[..., None] - cumulative)[..., None] * keys_in
    return (
        update_part,
        write_part,
        attend,
        growth[..., None] * queries,
        carried_keys,
        jnp.exp(final_sum),
    )


def advance(current_state, incoming_value_rows, carried_keys, decay_total):
    return decay_total[..., None, None] * current_state + jnp.einsum(
        "...ck,...cv->...kv", carried_keys, incoming_value_rows, precision=HIGH_PRECISION
    )


def pair_update(passed_block_state, inputs):
    current_update, current_write, carried_now, decay_now = inputs
    target_values = jnp.concatenate([current_update, jnp.zeros_like(current_update)], axis=-1)
    incoming_value_rows = target_values - jnp.einsum(
        "zsg,zgj->zsj", current_write, passed_block_state, precision=HIGH_PRECISION
    )
    return advance(passed_block_state, incoming_value_rows, carried_now, decay_now)


def shifted(value, axis, steps):
    count = lax.axis_size(axis)
    return lax.ppermute(value, axis, [(source, source + steps) for source in range(count - steps)])


def incoming_state(pair, axis):
    count = lax.axis_size(axis)
    place = lax.axis_index(axis)
    state = pair[..., :HD]
    if count == 1:
        return jnp.zeros_like(state)
    width = 1
    while 2 * width < count:
        got = shifted(pair, axis, width)
        joined = jnp.einsum("hij,hjk->hik", pair[..., HD:], got, precision=HIGH_PRECISION)
        joined = joined + jnp.concatenate([pair[..., :HD], jnp.zeros_like(state)], axis=-1)
        pair = jnp.where(place >= width, joined, pair)
        width *= 2
    previous = shifted(pair, axis, 1)
    result = previous[..., :HD]
    if width + 1 < count:
        far_state = shifted(pair[..., :HD], axis, width + 1)
        result = result + jnp.einsum(
            "hij,hjk->hik", previous[..., HD:], far_state, precision=HIGH_PRECISION
        )
    return result


def step_pair(pair, inputs):
    return (pair_update(pair, inputs), pair)


def group_output(mixed, gate_share, decay_log, dt_bias, norm_gain):
    queries, keys_in, values_in, beta_gate, log_decay = split_heads(
        mixed, gate_share, decay_log, dt_bias
    )
    update_part, write_part, attend, grown_query, carried_keys, decay_total = block_terms(
        queries, keys_in, values_in, beta_gate, log_decay
    )
    head_count = queries.shape[1]
    zero_state = jnp.zeros((head_count, HD, HD), jnp.float32)
    identity = jnp.broadcast_to(jnp.eye(HD, dtype=jnp.float32), (head_count, HD, HD))
    start_pair = jnp.concatenate([zero_state, identity], axis=-1)
    sequence = (update_part, write_part, carried_keys, decay_total)
    final_pair, start_pairs = lax.scan(step_pair, start_pair, sequence)
    incoming = incoming_state(final_pair, "outer")
    effective_query = grown_query - jnp.einsum(
        "...ce,...ek->...ck", attend, write_part, precision=HIGH_PRECISION
    )
    local_part = jnp.einsum(
        "...ce,...ev->...cv", attend, update_part, precision=HIGH_PRECISION
    )
    through_state = jnp.einsum(
        "...ck,...kj->...cj", effective_query, start_pairs, precision=HIGH_PRECISION
    )
    local_part = local_part + through_state[..., :HD]
    outputs = local_part + jnp.einsum(
        "bhck,hkv->bhcv", through_state[..., HD:], incoming, precision=HIGH_PRECISION
    )
    scaled = (
        outputs
        * lax.rsqrt(jnp.mean(outputs * outputs, axis=-1, keepdims=True) + EPS_NORM)
        * norm_gain
    )
    normed = scaled.astype(jnp.bfloat16)
    return normed


def local(qkv_blocks, block_scales, gate_logits, conv_weight, decay_log, dt_bias, norm_gain):
    coded_share, scale_share, gate_share = (
        lax.all_to_all(qkv_blocks, "inner", split_axis=1, concat_axis=0, tiled=True),
        lax.all_to_all(block_scales, "inner", split_axis=1, concat_axis=0, tiled=True),
        lax.all_to_all(gate_logits, "inner", split_axis=1, concat_axis=0, tiled=True),
    )
    regrouped = dequantize(coded_share, scale_share)
    token_count = regrouped.shape[0]
    previous = from_behind(regrouped[token_count - CONV + 1 :], "outer", 1)
    mixed = convolve(jnp.concatenate([previous, regrouped], axis=0), conv_weight, token_count)
    key_share = mixed.shape[1]
    group_count = 2 if key_share % 2 == 0 else 1
    per_group = key_share // group_count
    pieces = []
    for group in range(group_count):
        keys_of = slice(group * per_group, (group + 1) * per_group)
        values_of = slice(2 * group * per_group, 2 * (group + 1) * per_group)
        pieces.append(
            group_output(
                mixed[:, keys_of],
                gate_share[:, keys_of],
                decay_log[values_of],
                dt_bias[values_of],
                norm_gain,
            )
        )
    normed = jnp.concatenate(pieces, axis=1)
    head_count = normed.shape[1]
    by_token = jnp.swapaxes(normed, 1, 2).reshape(token_count, head_count, HD)
    return lax.all_to_all(by_token, "inner", split_axis=0, concat_axis=1, tiled=True)


def solution(mesh):
    placed = (
        P(("outer", "inner"), None, None),
        P(("outer", "inner"), None, None),
        P(("outer", "inner"), None, None),
        P(None, "inner", None),
        P("inner"),
        P("inner"),
        P(),
    )
    return jax.shard_map(
        local,
        mesh=mesh,
        in_specs=placed,
        out_specs=P(("outer", "inner"), None, None),
        check_vma=False,
    )
```

```python
import jax
import jax.numpy as jnp
from jax import lax
from jax.sharding import PartitionSpec as P

HD = 128
BLOCK = 128
QB = 32
CONV = 4


HIGH_PRECISION = lax.Precision.HIGH
EPS_NORM = 1e-06


def from_behind(value, axis, steps):
    count = lax.axis_size(axis)
    leading, last = (max(0, -steps), min(count, count - steps))
    return lax.ppermute(value, axis, [(source, source + steps) for source in range(leading, last)])


def dequantize(blocks, scales):
    token_count = blocks.shape[0]
    channels = blocks.shape[2]
    quarter = channels // 4
    per_token = jnp.repeat(scales.astype(jnp.float32), QB, axis=0)
    group = lax.broadcasted_iota(jnp.int32, (1, 1, channels), 2) // quarter
    spread = jnp.broadcast_to(per_token[..., 0:1], blocks.shape)
    for part in range(1, 4):
        spread = jnp.where(group == part, per_token[..., part : part + 1], spread)
    return blocks.astype(jnp.float32) * spread


def convolve(extended, conv_weight, token_count):
    summed = conv_weight[0] * extended[0:token_count]
    for offset in range(1, CONV):
        summed = summed + conv_weight[offset] * extended[offset : offset + token_count]
    return jax.nn.silu(summed)


def unit_rows(matrix):
    return matrix * lax.rsqrt(jnp.sum(matrix * matrix, axis=-1, keepdims=True) + EPS_NORM)


def split_heads(mixed, gate_share, decay_log, dt_bias):
    token_count = mixed.shape[0]
    value_heads = 2 * mixed.shape[1]
    block_count = token_count // BLOCK
    queries = jnp.repeat(unit_rows(mixed[:, :, :HD]), 2, axis=1)
    keys_in = jnp.repeat(unit_rows(mixed[:, :, HD : 2 * HD]), 2, axis=1)
    values_in = mixed[:, :, 2 * HD :].reshape(token_count, value_heads, HD)
    gate_values = gate_share.astype(jnp.float32)
    beta_gate = jax.nn.sigmoid(gate_values[:, :, :2].reshape(token_count, value_heads))
    raw_decay = gate_values[:, :, 2:].reshape(token_count, value_heads)
    log_decay = -jnp.exp(decay_log) * jax.nn.softplus(raw_decay + dt_bias)

    def blocked(tensor):
        return jnp.swapaxes(tensor.reshape((block_count, BLOCK) + tensor.shape[1:]), 1, 2)

    return (
        blocked(queries),
        blocked(keys_in),
        blocked(values_in),
        blocked(beta_gate),
        blocked(log_decay),
    )


def lower_inverse(strict_part, length):
    negated = -strict_part
    eye_block = jnp.eye(length, dtype=jnp.float32)
    inverse = eye_block + negated
    power = negated
    for unused_level in range((length - 1).bit_length() - 1):
        power = jnp.einsum("...ij,...jk->...ik", power, power, precision=HIGH_PRECISION)
        inverse = inverse + jnp.einsum(
            "...ij,...jk->...ik", inverse, power, precision=HIGH_PRECISION
        )
    return inverse


def block_terms(queries, keys_in, values_in, beta_gate, log_decay):
    cumulative = jnp.cumsum(log_decay, axis=-1)
    length = log_decay.shape[-1]
    row_index = lax.broadcasted_iota(jnp.int32, (length, length), 0)
    col_index = lax.broadcasted_iota(jnp.int32, (length, length), 1)
    lower_mask = row_index >= col_index
    strict = row_index > col_index
    differ = cumulative[..., :, None] - cumulative[..., None, :]
    weights = jnp.where(lower_mask, jnp.exp(jnp.where(lower_mask, differ, 0.0)), 0.0)
    key_dots = jnp.einsum("...cd,...ed->...ce", keys_in, keys_in, precision=HIGH_PRECISION)
    strict_part = jnp.where(strict, key_dots * weights * beta_gate[..., :, None], 0.0)
    growth = jnp.exp(cumulative)
    right_side = jnp.concatenate(
        [beta_gate[..., None] * values_in, (beta_gate * growth)[..., None] * keys_in], axis=-1
    )
    inverse = lower_inverse(strict_part, length)
    solved = jnp.einsum("...ce,...ed->...cd", inverse, right_side, precision=HIGH_PRECISION)
    head_width = values_in.shape[-1]
    update_part = solved[..., :head_width]
    write_part = solved[..., head_width:]
    attend = jnp.einsum("...cd,...ed->...ce", queries, keys_in, precision=HIGH_PRECISION) * weights
    final_sum = cumulative[..., -1]
    carried_keys = jnp.exp(final_sum[..., None] - cumulative)[..., None] * keys_in
    return (
        update_part,
        write_part,
        attend,
        growth[..., None] * queries,
        carried_keys,
        jnp.exp(final_sum),
    )


def advance(current_state, incoming_value_rows, carried_keys, decay_total):
    return decay_total[..., None, None] * current_state + jnp.einsum(
        "...ck,...cv->...kv", carried_keys, incoming_value_rows, precision=HIGH_PRECISION
    )


def pair_update(passed_block_state, inputs):
    current_update, current_write, carried_now, decay_now = inputs
    target_values = jnp.concatenate([current_update, jnp.zeros_like(current_update)], axis=-1)
    incoming_value_rows = target_values - jnp.einsum(
        "zsg,zgj->zsj", current_write, passed_block_state, precision=HIGH_PRECISION
    )
    return advance(passed_block_state, incoming_value_rows, carried_now, decay_now)


def shifted(value, axis, steps):
    count = lax.axis_size(axis)
    return lax.ppermute(value, axis, [(source, source + steps) for source in range(count - steps)])


def incoming_state(pair, axis):
    count = lax.axis_size(axis)
    place = lax.axis_index(axis)
    state = pair[..., :HD]
    if count == 1:
        return jnp.zeros_like(state)
    width = 1
    while 2 * width < count:
        got = shifted(pair, axis, width)
        joined = jnp.einsum("hij,hjk->hik", pair[..., HD:], got, precision=HIGH_PRECISION)
        joined = joined + jnp.concatenate([pair[..., :HD], jnp.zeros_like(state)], axis=-1)
        pair = jnp.where(place >= width, joined, pair)
        width *= 2
    previous = shifted(pair, axis, 1)
    result = previous[..., :HD]
    if width + 1 < count:
        far_state = shifted(pair[..., :HD], axis, width + 1)
        result = result + jnp.einsum(
            "hij,hjk->hik", previous[..., HD:], far_state, precision=HIGH_PRECISION
        )
    return result


def step_pair(pair, inputs):
    return (pair_update(pair, inputs), pair)


def local(qkv_blocks, block_scales, gate_logits, conv_weight, decay_log, dt_bias, norm_gain):
    coded_share, scale_share, gate_share = (
        lax.all_to_all(qkv_blocks, "inner", split_axis=1, concat_axis=0, tiled=True),
        lax.all_to_all(block_scales, "inner", split_axis=1, concat_axis=0, tiled=True),
        lax.all_to_all(gate_logits, "inner", split_axis=1, concat_axis=0, tiled=True),
    )
    regrouped = dequantize(coded_share, scale_share)
    token_count = regrouped.shape[0]
    previous = from_behind(regrouped[token_count - CONV + 1 :], "outer", 1)
    mixed = convolve(jnp.concatenate([previous, regrouped], axis=0), conv_weight, token_count)
    queries, keys_in, values_in, beta_gate, log_decay = split_heads(
        mixed, gate_share, decay_log, dt_bias
    )
    update_part, write_part, attend, grown_query, carried_keys, decay_total = block_terms(
        queries, keys_in, values_in, beta_gate, log_decay
    )
    head_count = queries.shape[1]
    zero_state = jnp.zeros((head_count, HD, HD), jnp.float32)
    identity = jnp.broadcast_to(jnp.eye(HD, dtype=jnp.float32), (head_count, HD, HD))
    start_pair = jnp.concatenate([zero_state, identity], axis=-1)
    sequence = (update_part, write_part, carried_keys, decay_total)
    final_pair, start_pairs = lax.scan(step_pair, start_pair, sequence)
    incoming = incoming_state(final_pair, "outer")
    effective_query = grown_query - jnp.einsum(
        "...ce,...ek->...ck", attend, write_part, precision=HIGH_PRECISION
    )
    local_part = jnp.einsum(
        "...ce,...ev->...cv", attend, update_part, precision=HIGH_PRECISION
    )
    through_state = jnp.einsum(
        "...ck,...kj->...cj", effective_query, start_pairs, precision=HIGH_PRECISION
    )
    local_part = local_part + through_state[..., :HD]
    outputs = local_part + jnp.einsum(
        "bhck,hkv->bhcv", through_state[..., HD:], incoming, precision=HIGH_PRECISION
    )
    scaled = (
        outputs
        * lax.rsqrt(jnp.mean(outputs * outputs, axis=-1, keepdims=True) + EPS_NORM)
        * norm_gain
    )
    normed = scaled.astype(jnp.bfloat16)
    by_token = jnp.swapaxes(normed, 1, 2).reshape(token_count, head_count, HD)
    return lax.all_to_all(by_token, "inner", split_axis=0, concat_axis=1, tiled=True)


def solution(mesh):
    placed = (
        P(("outer", "inner"), None, None),
        P(("outer", "inner"), None, None),
        P(("outer", "inner"), None, None),
        P(None, "inner", None),
        P("inner"),
        P("inner"),
        P(),
    )
    return jax.shard_map(
        local,
        mesh=mesh,
        in_specs=placed,
        out_specs=P(("outer", "inner"), None, None),
        check_vma=False,
    )
```

```python
import jax
import jax.numpy as jnp
from jax import lax
from jax.sharding import PartitionSpec as P

HD = 128
BLOCK = 128
QB = 32
CONV = 4


HIGH_PRECISION = lax.Precision.HIGHEST
FAST_PRECISION = lax.Precision.HIGH
EPS_NORM = 1e-06


def from_behind(value, axis, steps):
    count = lax.axis_size(axis)
    leading, last = (max(0, -steps), min(count, count - steps))
    return lax.ppermute(value, axis, [(source, source + steps) for source in range(leading, last)])


def dequantize(blocks, scales):
    token_count = blocks.shape[0]
    channels = blocks.shape[2]
    quarter = channels // 4
    per_token = jnp.repeat(scales.astype(jnp.float32), QB, axis=0)
    group = lax.broadcasted_iota(jnp.int32, (1, 1, channels), 2) // quarter
    spread = jnp.broadcast_to(per_token[..., 0:1], blocks.shape)
    for part in range(1, 4):
        spread = jnp.where(group == part, per_token[..., part : part + 1], spread)
    return blocks.astype(jnp.float32) * spread


def convolve(extended, conv_weight, token_count):
    summed = conv_weight[0] * extended[0:token_count]
    for offset in range(1, CONV):
        summed = summed + conv_weight[offset] * extended[offset : offset + token_count]
    return jax.nn.silu(summed)


def unit_rows(matrix):
    return matrix * lax.rsqrt(jnp.sum(matrix * matrix, axis=-1, keepdims=True) + EPS_NORM)


def split_heads(mixed, gate_share, decay_log, dt_bias):
    token_count = mixed.shape[0]
    value_heads = 2 * mixed.shape[1]
    block_count = token_count // BLOCK
    queries = jnp.repeat(unit_rows(mixed[:, :, :HD]), 2, axis=1)
    keys_in = jnp.repeat(unit_rows(mixed[:, :, HD : 2 * HD]), 2, axis=1)
    values_in = mixed[:, :, 2 * HD :].reshape(token_count, value_heads, HD)
    gate_values = gate_share.astype(jnp.float32)
    beta_gate = jax.nn.sigmoid(gate_values[:, :, :2].reshape(token_count, value_heads))
    raw_decay = gate_values[:, :, 2:].reshape(token_count, value_heads)
    log_decay = -jnp.exp(decay_log) * jax.nn.softplus(raw_decay + dt_bias)

    def blocked(tensor):
        return jnp.swapaxes(tensor.reshape((block_count, BLOCK) + tensor.shape[1:]), 1, 2)

    return (
        blocked(queries),
        blocked(keys_in),
        blocked(values_in),
        blocked(beta_gate),
        blocked(log_decay),
    )


def lower_inverse(strict_part, length):
    negated = -strict_part
    eye_block = jnp.eye(length, dtype=jnp.float32)
    inverse = eye_block + negated
    power = negated
    for unused_level in range((length - 1).bit_length() - 1):
        power = jnp.einsum("...ij,...jk->...ik", power, power, precision=FAST_PRECISION)
        inverse = inverse + jnp.einsum(
            "...ij,...jk->...ik", inverse, power, precision=FAST_PRECISION
        )
    return inverse


def block_terms(queries, keys_in, values_in, beta_gate, log_decay):
    cumulative = jnp.cumsum(log_decay, axis=-1)
    length = log_decay.shape[-1]
    row_index = lax.broadcasted_iota(jnp.int32, (length, length), 0)
    col_index = lax.broadcasted_iota(jnp.int32, (length, length), 1)
    lower_mask = row_index >= col_index
    strict = row_index > col_index
    differ = cumulative[..., :, None] - cumulative[..., None, :]
    weights = jnp.where(lower_mask, jnp.exp(jnp.where(lower_mask, differ, 0.0)), 0.0)
    key_dots = jnp.einsum("...cd,...ed->...ce", keys_in, keys_in, precision=HIGH_PRECISION)
    strict_part = jnp.where(strict, key_dots * weights * beta_gate[..., :, None], 0.0)
    growth = jnp.exp(cumulative)
    right_side = jnp.concatenate(
        [beta_gate[..., None] * values_in, (beta_gate * growth)[..., None] * keys_in], axis=-1
    )
    inverse = lower_inverse(strict_part, length)
    solved = jnp.einsum("...ce,...ed->...cd", inverse, right_side, precision=HIGH_PRECISION)
    head_width = values_in.shape[-1]
    update_part = solved[..., :head_width]
    write_part = solved[..., head_width:]
    attend = jnp.einsum("...cd,...ed->...ce", queries, keys_in, precision=HIGH_PRECISION) * weights
    final_sum = cumulative[..., -1]
    carried_keys = jnp.exp(final_sum[..., None] - cumulative)[..., None] * keys_in
    return (
        update_part,
        write_part,
        attend,
        growth[..., None] * queries,
        carried_keys,
        jnp.exp(final_sum),
    )


def advance(current_state, incoming_value_rows, carried_keys, decay_total):
    return decay_total[..., None, None] * current_state + jnp.einsum(
        "...ck,...cv->...kv", carried_keys, incoming_value_rows, precision=HIGH_PRECISION
    )


def pair_update(passed_block_state, inputs):
    current_update, current_write, carried_now, decay_now = inputs
    target_values = jnp.concatenate([current_update, jnp.zeros_like(current_update)], axis=-1)
    incoming_value_rows = target_values - jnp.einsum(
        "zsg,zgj->zsj", current_write, passed_block_state, precision=HIGH_PRECISION
    )
    return advance(passed_block_state, incoming_value_rows, carried_now, decay_now)


def shifted(value, axis, steps):
    count = lax.axis_size(axis)
    return lax.ppermute(value, axis, [(source, source + steps) for source in range(count - steps)])


def incoming_state(pair, axis):
    count = lax.axis_size(axis)
    place = lax.axis_index(axis)
    state = pair[..., :HD]
    if count == 1:
        return jnp.zeros_like(state)
    width = 1
    while 2 * width < count:
        got = shifted(pair, axis, width)
        joined = jnp.einsum("hij,hjk->hik", pair[..., HD:], got, precision=HIGH_PRECISION)
        joined = joined + jnp.concatenate([pair[..., :HD], jnp.zeros_like(state)], axis=-1)
        pair = jnp.where(place >= width, joined, pair)
        width *= 2
    previous = shifted(pair, axis, 1)
    result = previous[..., :HD]
    if width + 1 < count:
        far_state = shifted(pair[..., :HD], axis, width + 1)
        result = result + jnp.einsum(
            "hij,hjk->hik", previous[..., HD:], far_state, precision=HIGH_PRECISION
        )
    return result


def step_pair(pair, inputs):
    return (pair_update(pair, inputs), pair)


def local(qkv_blocks, block_scales, gate_logits, conv_weight, decay_log, dt_bias, norm_gain):
    coded_share, scale_share, gate_share = (
        lax.all_to_all(qkv_blocks, "inner", split_axis=1, concat_axis=0, tiled=True),
        lax.all_to_all(block_scales, "inner", split_axis=1, concat_axis=0, tiled=True),
        lax.all_to_all(gate_logits, "inner", split_axis=1, concat_axis=0, tiled=True),
    )
    regrouped = dequantize(coded_share, scale_share)
    token_count = regrouped.shape[0]
    previous = from_behind(regrouped[token_count - CONV + 1 :], "outer", 1)
    mixed = convolve(jnp.concatenate([previous, regrouped], axis=0), conv_weight, token_count)
    queries, keys_in, values_in, beta_gate, log_decay = split_heads(
        mixed, gate_share, decay_log, dt_bias
    )
    update_part, write_part, attend, grown_query, carried_keys, decay_total = block_terms(
        queries, keys_in, values_in, beta_gate, log_decay
    )
    head_count = queries.shape[1]
    zero_state = jnp.zeros((head_count, HD, HD), jnp.float32)
    identity = jnp.broadcast_to(jnp.eye(HD, dtype=jnp.float32), (head_count, HD, HD))
    start_pair = jnp.concatenate([zero_state, identity], axis=-1)
    sequence = (update_part, write_part, carried_keys, decay_total)
    final_pair, start_pairs = lax.scan(step_pair, start_pair, sequence)
    incoming = incoming_state(final_pair, "outer")
    effective_query = grown_query - jnp.einsum(
        "...ce,...ek->...ck", attend, write_part, precision=HIGH_PRECISION
    )
    local_part = jnp.einsum(
        "...ce,...ev->...cv", attend, update_part, precision=HIGH_PRECISION
    )
    through_state = jnp.einsum(
        "...ck,...kj->...cj", effective_query, start_pairs, precision=HIGH_PRECISION
    )
    local_part = local_part + through_state[..., :HD]
    outputs = local_part + jnp.einsum(
        "bhck,hkv->bhcv", through_state[..., HD:], incoming, precision=HIGH_PRECISION
    )
    scaled = (
        outputs
        * lax.rsqrt(jnp.mean(outputs * outputs, axis=-1, keepdims=True) + EPS_NORM)
        * norm_gain
    )
    normed = scaled.astype(jnp.bfloat16)
    by_token = jnp.swapaxes(normed, 1, 2).reshape(token_count, head_count, HD)
    return lax.all_to_all(by_token, "inner", split_axis=0, concat_axis=1, tiled=True)


def solution(mesh):
    placed = (
        P(("outer", "inner"), None, None),
        P(("outer", "inner"), None, None),
        P(("outer", "inner"), None, None),
        P(None, "inner", None),
        P("inner"),
        P("inner"),
        P(),
    )
    return jax.shard_map(
        local,
        mesh=mesh,
        in_specs=placed,
        out_specs=P(("outer", "inner"), None, None),
        check_vma=False,
    )
```

```python
import jax
import jax.numpy as jnp
from jax import lax
from jax.sharding import PartitionSpec as P

HD = 128
BLOCK = 128
QB = 32
CONV = 4


HIGH_PRECISION = lax.Precision.HIGHEST
FAST_PRECISION = lax.Precision.HIGH
EPS_NORM = 1e-06


def from_behind(value, axis, steps):
    count = lax.axis_size(axis)
    leading, last = (max(0, -steps), min(count, count - steps))
    return lax.ppermute(value, axis, [(source, source + steps) for source in range(leading, last)])


def dequantize(blocks, scales):
    token_count = blocks.shape[0]
    channels = blocks.shape[2]
    quarter = channels // 4
    per_token = jnp.repeat(scales.astype(jnp.float32), QB, axis=0)
    group = lax.broadcasted_iota(jnp.int32, (1, 1, channels), 2) // quarter
    spread = jnp.broadcast_to(per_token[..., 0:1], blocks.shape)
    for part in range(1, 4):
        spread = jnp.where(group == part, per_token[..., part : part + 1], spread)
    return blocks.astype(jnp.float32) * spread


def convolve(extended, conv_weight, token_count):
    summed = conv_weight[0] * extended[0:token_count]
    for offset in range(1, CONV):
        summed = summed + conv_weight[offset] * extended[offset : offset + token_count]
    return jax.nn.silu(summed)


def unit_rows(matrix):
    return matrix * lax.rsqrt(jnp.sum(matrix * matrix, axis=-1, keepdims=True) + EPS_NORM)


def split_heads(mixed, gate_share, decay_log, dt_bias):
    token_count = mixed.shape[0]
    value_heads = 2 * mixed.shape[1]
    block_count = token_count // BLOCK
    queries = jnp.repeat(unit_rows(mixed[:, :, :HD]), 2, axis=1)
    keys_in = jnp.repeat(unit_rows(mixed[:, :, HD : 2 * HD]), 2, axis=1)
    values_in = mixed[:, :, 2 * HD :].reshape(token_count, value_heads, HD)
    gate_values = gate_share.astype(jnp.float32)
    beta_gate = jax.nn.sigmoid(gate_values[:, :, :2].reshape(token_count, value_heads))
    raw_decay = gate_values[:, :, 2:].reshape(token_count, value_heads)
    log_decay = -jnp.exp(decay_log) * jax.nn.softplus(raw_decay + dt_bias)

    def blocked(tensor):
        return jnp.swapaxes(tensor.reshape((block_count, BLOCK) + tensor.shape[1:]), 1, 2)

    return (
        blocked(queries),
        blocked(keys_in),
        blocked(values_in),
        blocked(beta_gate),
        blocked(log_decay),
    )


def lower_inverse(strict_part, length):
    negated = -strict_part
    eye_block = jnp.eye(length, dtype=jnp.float32)
    inverse = eye_block + negated
    power = negated
    for unused_level in range((length - 1).bit_length() - 1):
        power = jnp.einsum("...ij,...jk->...ik", power, power, precision=FAST_PRECISION)
        inverse = inverse + jnp.einsum(
            "...ij,...jk->...ik", inverse, power, precision=FAST_PRECISION
        )
    return inverse


def block_terms(queries, keys_in, values_in, beta_gate, log_decay):
    cumulative = jnp.cumsum(log_decay, axis=-1)
    length = log_decay.shape[-1]
    row_index = lax.broadcasted_iota(jnp.int32, (length, length), 0)
    col_index = lax.broadcasted_iota(jnp.int32, (length, length), 1)
    lower_mask = row_index >= col_index
    strict = row_index > col_index
    differ = cumulative[..., :, None] - cumulative[..., None, :]
    weights = jnp.where(lower_mask, jnp.exp(jnp.where(lower_mask, differ, 0.0)), 0.0)
    key_dots = jnp.einsum("...cd,...ed->...ce", keys_in, keys_in, precision=HIGH_PRECISION)
    strict_part = jnp.where(strict, key_dots * weights * beta_gate[..., :, None], 0.0)
    growth = jnp.exp(cumulative)
    right_side = jnp.concatenate(
        [beta_gate[..., None] * values_in, (beta_gate * growth)[..., None] * keys_in], axis=-1
    )
    inverse = lower_inverse(strict_part, length)
    solved = jnp.einsum("...ce,...ed->...cd", inverse, right_side, precision=HIGH_PRECISION)
    head_width = values_in.shape[-1]
    update_part = solved[..., :head_width]
    write_part = solved[..., head_width:]
    attend = jnp.einsum("...cd,...ed->...ce", queries, keys_in, precision=HIGH_PRECISION) * weights
    final_sum = cumulative[..., -1]
    carried_keys = jnp.exp(final_sum[..., None] - cumulative)[..., None] * keys_in
    return (
        update_part,
        write_part,
        attend,
        growth[..., None] * queries,
        carried_keys,
        jnp.exp(final_sum),
    )


def shifted(value, axis, steps):
    count = lax.axis_size(axis)
    return lax.ppermute(value, axis, [(source, source + steps) for source in range(count - steps)])


def incoming_state(pair, axis):
    count = lax.axis_size(axis)
    place = lax.axis_index(axis)
    state = pair[..., :HD]
    if count == 1:
        return jnp.zeros_like(state)
    width = 1
    while 2 * width < count:
        got = shifted(pair, axis, width)
        joined = jnp.einsum("hij,hjk->hik", pair[..., HD:], got, precision=HIGH_PRECISION)
        joined = joined + jnp.concatenate([pair[..., :HD], jnp.zeros_like(state)], axis=-1)
        pair = jnp.where(place >= width, joined, pair)
        width *= 2
    previous = shifted(pair, axis, 1)
    result = previous[..., :HD]
    if width + 1 < count:
        far_state = shifted(pair[..., :HD], axis, width + 1)
        result = result + jnp.einsum(
            "hij,hjk->hik", previous[..., HD:], far_state, precision=HIGH_PRECISION
        )
    return result


def compose_pairs(earlier, later):
    moved = jnp.einsum("...ij,...jk->...ik", later[..., HD:], earlier, precision=HIGH_PRECISION)
    return moved + jnp.concatenate([later[..., :HD], jnp.zeros_like(later[..., :HD])], axis=-1)


def local(qkv_blocks, block_scales, gate_logits, conv_weight, decay_log, dt_bias, norm_gain):
    coded_share, scale_share, gate_share = (
        lax.all_to_all(qkv_blocks, "inner", split_axis=1, concat_axis=0, tiled=True),
        lax.all_to_all(block_scales, "inner", split_axis=1, concat_axis=0, tiled=True),
        lax.all_to_all(gate_logits, "inner", split_axis=1, concat_axis=0, tiled=True),
    )
    regrouped = dequantize(coded_share, scale_share)
    token_count = regrouped.shape[0]
    previous = from_behind(regrouped[token_count - CONV + 1 :], "outer", 1)
    mixed = convolve(jnp.concatenate([previous, regrouped], axis=0), conv_weight, token_count)
    queries, keys_in, values_in, beta_gate, log_decay = split_heads(
        mixed, gate_share, decay_log, dt_bias
    )
    update_part, write_part, attend, grown_query, carried_keys, decay_total = block_terms(
        queries, keys_in, values_in, beta_gate, log_decay
    )
    head_count = queries.shape[1]
    zero_state = jnp.zeros((head_count, HD, HD), jnp.float32)
    identity = jnp.broadcast_to(jnp.eye(HD, dtype=jnp.float32), (head_count, HD, HD))
    start_pair = jnp.concatenate([zero_state, identity], axis=-1)
    target = jnp.concatenate([update_part, -write_part], axis=-1)
    pairs = jnp.einsum("...ck,...cj->...kj", carried_keys, target, precision=HIGH_PRECISION)
    pairs = pairs + jnp.concatenate(
        [jnp.zeros_like(update_part), decay_total[..., None, None] * identity], axis=-1
    )
    block_count = pairs.shape[0]
    distance = 1
    while distance < block_count:
        joined = compose_pairs(pairs[:-distance], pairs[distance:])
        pairs = jnp.concatenate([pairs[:distance], joined], axis=0)
        distance *= 2
    final_pair = pairs[-1]
    start_pairs = jnp.concatenate([start_pair[None], pairs[:-1]], axis=0)
    incoming = incoming_state(final_pair, "outer")
    effective_query = grown_query - jnp.einsum(
        "...ce,...ek->...ck", attend, write_part, precision=HIGH_PRECISION
    )
    local_part = jnp.einsum(
        "...ce,...ev->...cv", attend, update_part, precision=HIGH_PRECISION
    )
    through_state = jnp.einsum(
        "...ck,...kj->...cj", effective_query, start_pairs, precision=HIGH_PRECISION
    )
    local_part = local_part + through_state[..., :HD]
    outputs = local_part + jnp.einsum(
        "bhck,hkv->bhcv", through_state[..., HD:], incoming, precision=HIGH_PRECISION
    )
    scaled = (
        outputs
        * lax.rsqrt(jnp.mean(outputs * outputs, axis=-1, keepdims=True) + EPS_NORM)
        * norm_gain
    )
    normed = scaled.astype(jnp.bfloat16)
    by_token = jnp.swapaxes(normed, 1, 2).reshape(token_count, head_count, HD)
    return lax.all_to_all(by_token, "inner", split_axis=0, concat_axis=1, tiled=True)


def solution(mesh):
    placed = (
        P(("outer", "inner"), None, None),
        P(("outer", "inner"), None, None),
        P(("outer", "inner"), None, None),
        P(None, "inner", None),
        P("inner"),
        P("inner"),
        P(),
    )
    return jax.shard_map(
        local,
        mesh=mesh,
        in_specs=placed,
        out_specs=P(("outer", "inner"), None, None),
        check_vma=False,
    )
```

```python
import jax
import jax.numpy as jnp
from jax import lax
from jax.sharding import PartitionSpec as P

HD = 128
BLOCK = 128
QB = 32
CONV = 4


HIGH_PRECISION = lax.Precision.HIGHEST
FAST_PRECISION = lax.Precision.HIGH
EPS_NORM = 1e-06


def from_behind(value, axis, steps):
    count = lax.axis_size(axis)
    leading, last = (max(0, -steps), min(count, count - steps))
    return lax.ppermute(value, axis, [(source, source + steps) for source in range(leading, last)])


def dequantize(blocks, scales):
    token_count = blocks.shape[0]
    channels = blocks.shape[2]
    quarter = channels // 4
    per_token = jnp.repeat(scales.astype(jnp.float32), QB, axis=0)
    group = lax.broadcasted_iota(jnp.int32, (1, 1, channels), 2) // quarter
    spread = jnp.broadcast_to(per_token[..., 0:1], blocks.shape)
    for part in range(1, 4):
        spread = jnp.where(group == part, per_token[..., part : part + 1], spread)
    return blocks.astype(jnp.float32) * spread


def convolve(extended, conv_weight, token_count):
    summed = conv_weight[0] * extended[0:token_count]
    for offset in range(1, CONV):
        summed = summed + conv_weight[offset] * extended[offset : offset + token_count]
    return jax.nn.silu(summed)


def unit_rows(matrix):
    return matrix * lax.rsqrt(jnp.sum(matrix * matrix, axis=-1, keepdims=True) + EPS_NORM)


def split_heads(mixed, gate_share, decay_log, dt_bias):
    token_count = mixed.shape[0]
    value_heads = 2 * mixed.shape[1]
    block_count = token_count // BLOCK
    queries = jnp.repeat(unit_rows(mixed[:, :, :HD]), 2, axis=1)
    keys_in = jnp.repeat(unit_rows(mixed[:, :, HD : 2 * HD]), 2, axis=1)
    values_in = mixed[:, :, 2 * HD :].reshape(token_count, value_heads, HD)
    gate_values = gate_share.astype(jnp.float32)
    beta_gate = jax.nn.sigmoid(gate_values[:, :, :2].reshape(token_count, value_heads))
    raw_decay = gate_values[:, :, 2:].reshape(token_count, value_heads)
    log_decay = -jnp.exp(decay_log) * jax.nn.softplus(raw_decay + dt_bias)

    def blocked(tensor):
        return jnp.swapaxes(tensor.reshape((block_count, BLOCK) + tensor.shape[1:]), 1, 2)

    return (
        blocked(queries),
        blocked(keys_in),
        blocked(values_in),
        blocked(beta_gate),
        blocked(log_decay),
    )


def lower_inverse(strict_part, length):
    negated = lax.optimization_barrier(-strict_part)
    eye_block = jnp.eye(length, dtype=jnp.float32)
    inverse = eye_block + negated
    power = negated
    for unused_level in range((length - 1).bit_length() - 1):
        power = jnp.einsum("...ij,...jk->...ik", power, power, precision=FAST_PRECISION)
        inverse = inverse + jnp.einsum(
            "...ij,...jk->...ik", inverse, power, precision=FAST_PRECISION
        )
    return inverse


def block_terms(queries, keys_in, values_in, beta_gate, log_decay):
    cumulative = jnp.cumsum(log_decay, axis=-1)
    length = log_decay.shape[-1]
    row_index = lax.broadcasted_iota(jnp.int32, (length, length), 0)
    col_index = lax.broadcasted_iota(jnp.int32, (length, length), 1)
    lower_mask = row_index >= col_index
    strict = row_index > col_index
    differ = cumulative[..., :, None] - cumulative[..., None, :]
    weights = jnp.where(lower_mask, jnp.exp(jnp.where(lower_mask, differ, 0.0)), 0.0)
    key_dots = jnp.einsum("...cd,...ed->...ce", keys_in, keys_in, precision=HIGH_PRECISION)
    strict_part = jnp.where(strict, key_dots * weights * beta_gate[..., :, None], 0.0)
    growth = jnp.exp(cumulative)
    right_side = jnp.concatenate(
        [beta_gate[..., None] * values_in, (beta_gate * growth)[..., None] * keys_in], axis=-1
    )
    inverse = lower_inverse(strict_part, length)
    solved = jnp.einsum("...ce,...ed->...cd", inverse, right_side, precision=HIGH_PRECISION)
    head_width = values_in.shape[-1]
    update_part = solved[..., :head_width]
    write_part = solved[..., head_width:]
    attend = jnp.einsum("...cd,...ed->...ce", queries, keys_in, precision=HIGH_PRECISION) * weights
    final_sum = cumulative[..., -1]
    carried_keys = jnp.exp(final_sum[..., None] - cumulative)[..., None] * keys_in
    return (
        update_part,
        write_part,
        attend,
        growth[..., None] * queries,
        carried_keys,
        jnp.exp(final_sum),
    )


def shifted(value, axis, steps):
    count = lax.axis_size(axis)
    return lax.ppermute(value, axis, [(source, source + steps) for source in range(count - steps)])


def incoming_state(pair, axis):
    count = lax.axis_size(axis)
    place = lax.axis_index(axis)
    state = pair[..., :HD]
    if count == 1:
        return jnp.zeros_like(state)
    width = 1
    while 2 * width < count:
        got = shifted(pair, axis, width)
        joined = jnp.einsum("hij,hjk->hik", pair[..., HD:], got, precision=HIGH_PRECISION)
        joined = joined + jnp.concatenate([pair[..., :HD], jnp.zeros_like(state)], axis=-1)
        pair = jnp.where(place >= width, joined, pair)
        width *= 2
    previous = shifted(pair, axis, 1)
    result = previous[..., :HD]
    if width + 1 < count:
        far_state = shifted(pair[..., :HD], axis, width + 1)
        result = result + jnp.einsum(
            "hij,hjk->hik", previous[..., HD:], far_state, precision=HIGH_PRECISION
        )
    return result


def compose_pairs(earlier, later):
    moved = jnp.einsum("...ij,...jk->...ik", later[..., HD:], earlier, precision=HIGH_PRECISION)
    return moved + jnp.concatenate([later[..., :HD], jnp.zeros_like(later[..., :HD])], axis=-1)


def local(qkv_blocks, block_scales, gate_logits, conv_weight, decay_log, dt_bias, norm_gain):
    coded_share, scale_share, gate_share = (
        lax.all_to_all(qkv_blocks, "inner", split_axis=1, concat_axis=0, tiled=True),
        lax.all_to_all(block_scales, "inner", split_axis=1, concat_axis=0, tiled=True),
        lax.all_to_all(gate_logits, "inner", split_axis=1, concat_axis=0, tiled=True),
    )
    regrouped = dequantize(coded_share, scale_share)
    token_count = regrouped.shape[0]
    previous = from_behind(regrouped[token_count - CONV + 1 :], "outer", 1)
    mixed = convolve(jnp.concatenate([previous, regrouped], axis=0), conv_weight, token_count)
    queries, keys_in, values_in, beta_gate, log_decay = split_heads(
        mixed, gate_share, decay_log, dt_bias
    )
    update_part, write_part, attend, grown_query, carried_keys, decay_total = block_terms(
        queries, keys_in, values_in, beta_gate, log_decay
    )
    head_count = queries.shape[1]
    zero_state = jnp.zeros((head_count, HD, HD), jnp.float32)
    identity = jnp.broadcast_to(jnp.eye(HD, dtype=jnp.float32), (head_count, HD, HD))
    start_pair = jnp.concatenate([zero_state, identity], axis=-1)
    target = jnp.concatenate([update_part, -write_part], axis=-1)
    pairs = jnp.einsum("...ck,...cj->...kj", carried_keys, target, precision=HIGH_PRECISION)
    pairs = pairs + jnp.concatenate(
        [jnp.zeros_like(update_part), decay_total[..., None, None] * identity], axis=-1
    )
    block_count = pairs.shape[0]
    distance = 1
    while distance < block_count:
        joined = compose_pairs(pairs[:-distance], pairs[distance:])
        pairs = jnp.concatenate([pairs[:distance], joined], axis=0)
        distance *= 2
    final_pair = pairs[-1]
    start_pairs = jnp.concatenate([start_pair[None], pairs[:-1]], axis=0)
    incoming = incoming_state(final_pair, "outer")
    effective_query = grown_query - jnp.einsum(
        "...ce,...ek->...ck", attend, write_part, precision=HIGH_PRECISION
    )
    local_part = jnp.einsum(
        "...ce,...ev->...cv", attend, update_part, precision=HIGH_PRECISION
    )
    through_state = jnp.einsum(
        "...ck,...kj->...cj", effective_query, start_pairs, precision=HIGH_PRECISION
    )
    local_part = local_part + through_state[..., :HD]
    outputs = local_part + jnp.einsum(
        "bhck,hkv->bhcv", through_state[..., HD:], incoming, precision=HIGH_PRECISION
    )
    scaled = (
        outputs
        * lax.rsqrt(jnp.mean(outputs * outputs, axis=-1, keepdims=True) + EPS_NORM)
        * norm_gain
    )
    normed = scaled.astype(jnp.bfloat16)
    by_token = jnp.swapaxes(normed, 1, 2).reshape(token_count, head_count, HD)
    return lax.all_to_all(by_token, "inner", split_axis=0, concat_axis=1, tiled=True)


def solution(mesh):
    placed = (
        P(("outer", "inner"), None, None),
        P(("outer", "inner"), None, None),
        P(("outer", "inner"), None, None),
        P(None, "inner", None),
        P("inner"),
        P("inner"),
        P(),
    )
    return jax.shard_map(
        local,
        mesh=mesh,
        in_specs=placed,
        out_specs=P(("outer", "inner"), None, None),
        check_vma=False,
    )
```

```python
import jax
import jax.numpy as jnp
from jax import lax
from jax.sharding import PartitionSpec as P

HD = 128
BLOCK = 128
QB = 32
CONV = 4


HIGH_PRECISION = lax.Precision.HIGHEST
FAST_PRECISION = lax.Precision.HIGH
EPS_NORM = 1e-06


def from_behind(value, axis, steps):
    count = lax.axis_size(axis)
    leading, last = (max(0, -steps), min(count, count - steps))
    return lax.ppermute(value, axis, [(source, source + steps) for source in range(leading, last)])


def dequantize(blocks, scales):
    token_count = blocks.shape[0]
    channels = blocks.shape[2]
    quarter = channels // 4
    per_token = jnp.repeat(scales.astype(jnp.float32), QB, axis=0)
    group = lax.broadcasted_iota(jnp.int32, (1, 1, channels), 2) // quarter
    spread = jnp.broadcast_to(per_token[..., 0:1], blocks.shape)
    for part in range(1, 4):
        spread = jnp.where(group == part, per_token[..., part : part + 1], spread)
    return blocks.astype(jnp.float32) * spread


def convolve(extended, conv_weight, token_count):
    summed = conv_weight[0] * extended[0:token_count]
    for offset in range(1, CONV):
        summed = summed + conv_weight[offset] * extended[offset : offset + token_count]
    return jax.nn.silu(summed)


def unit_rows(matrix):
    return matrix * lax.rsqrt(jnp.sum(matrix * matrix, axis=-1, keepdims=True) + EPS_NORM)


def split_heads(mixed, gate_share, decay_log, dt_bias):
    token_count = mixed.shape[0]
    value_heads = 2 * mixed.shape[1]
    block_count = token_count // BLOCK
    queries = jnp.repeat(unit_rows(mixed[:, :, :HD]), 2, axis=1)
    keys_in = jnp.repeat(unit_rows(mixed[:, :, HD : 2 * HD]), 2, axis=1)
    values_in = mixed[:, :, 2 * HD :].reshape(token_count, value_heads, HD)
    gate_values = gate_share.astype(jnp.float32)
    beta_gate = jax.nn.sigmoid(gate_values[:, :, :2].reshape(token_count, value_heads))
    raw_decay = gate_values[:, :, 2:].reshape(token_count, value_heads)
    log_decay = -jnp.exp(decay_log) * jax.nn.softplus(raw_decay + dt_bias)

    def blocked(tensor):
        return jnp.swapaxes(tensor.reshape((block_count, BLOCK) + tensor.shape[1:]), 1, 2)

    return (
        blocked(queries),
        blocked(keys_in),
        blocked(values_in),
        blocked(beta_gate),
        blocked(log_decay),
    )


def lower_inverse(strict_part, length):
    negated = -strict_part
    eye_block = jnp.eye(length, dtype=jnp.float32)
    inverse = eye_block + negated
    power = negated
    for unused_level in range((length - 1).bit_length() - 1):
        power = jnp.einsum("...ij,...jk->...ik", power, power, precision=FAST_PRECISION)
        inverse = inverse + jnp.einsum(
            "...ij,...jk->...ik", inverse, power, precision=FAST_PRECISION
        )
    return inverse


def block_terms(queries, keys_in, values_in, beta_gate, log_decay):
    cumulative = jnp.cumsum(log_decay, axis=-1)
    length = log_decay.shape[-1]
    row_index = lax.broadcasted_iota(jnp.int32, (length, length), 0)
    col_index = lax.broadcasted_iota(jnp.int32, (length, length), 1)
    lower_mask = row_index >= col_index
    strict = row_index > col_index
    differ = cumulative[..., :, None] - cumulative[..., None, :]
    weights = jnp.where(lower_mask, jnp.exp(jnp.where(lower_mask, differ, 0.0)), 0.0)
    key_dots = jnp.einsum("...cd,...ed->...ce", keys_in, keys_in, precision=HIGH_PRECISION)
    strict_part = jnp.where(strict, key_dots * weights * beta_gate[..., :, None], 0.0)
    growth = jnp.exp(cumulative)
    right_side = jnp.concatenate(
        [beta_gate[..., None] * values_in, (beta_gate * growth)[..., None] * keys_in], axis=-1
    )
    inverse = lower_inverse(strict_part, length)
    solved = jnp.einsum("...ce,...ed->...cd", inverse, right_side, precision=HIGH_PRECISION)
    head_width = values_in.shape[-1]
    update_part = solved[..., :head_width]
    write_part = solved[..., head_width:]
    attend = jnp.einsum("...cd,...ed->...ce", queries, keys_in, precision=HIGH_PRECISION) * weights
    final_sum = cumulative[..., -1]
    carried_keys = jnp.exp(final_sum[..., None] - cumulative)[..., None] * keys_in
    return (
        update_part,
        write_part,
        attend,
        growth[..., None] * queries,
        carried_keys,
        jnp.exp(final_sum),
    )


def advance(current_state, incoming_value_rows, carried_keys, decay_total):
    return decay_total[..., None, None] * current_state + jnp.einsum(
        "...ck,...cv->...kv", carried_keys, incoming_value_rows, precision=HIGH_PRECISION
    )


def pair_update(passed_block_state, inputs):
    current_update, current_write, carried_now, decay_now = inputs
    target_values = jnp.concatenate([current_update, jnp.zeros_like(current_update)], axis=-1)
    incoming_value_rows = target_values - jnp.einsum(
        "zsg,zgj->zsj", current_write, passed_block_state, precision=HIGH_PRECISION
    )
    return advance(passed_block_state, incoming_value_rows, carried_now, decay_now)


def shifted(value, axis, steps):
    count = lax.axis_size(axis)
    return lax.ppermute(value, axis, [(source, source + steps) for source in range(count - steps)])


def incoming_state(pair, axis):
    count = lax.axis_size(axis)
    place = lax.axis_index(axis)
    state = pair[..., :HD]
    if count == 1:
        return jnp.zeros_like(state)
    width = 1
    while 2 * width < count:
        got = shifted(pair, axis, width)
        joined = jnp.einsum("hij,hjk->hik", pair[..., HD:], got, precision=HIGH_PRECISION)
        joined = joined + jnp.concatenate([pair[..., :HD], jnp.zeros_like(state)], axis=-1)
        pair = jnp.where(place >= width, joined, pair)
        width *= 2
    previous = shifted(pair, axis, 1)
    result = previous[..., :HD]
    if width + 1 < count:
        far_state = shifted(pair[..., :HD], axis, width + 1)
        result = result + jnp.einsum(
            "hij,hjk->hik", previous[..., HD:], far_state, precision=HIGH_PRECISION
        )
    return result


def step_pair(pair, inputs):
    return (pair_update(pair, inputs), pair)


def local(qkv_blocks, block_scales, gate_logits, conv_weight, decay_log, dt_bias, norm_gain):
    coded_share, scale_share, gate_share = (
        lax.all_to_all(qkv_blocks, "inner", split_axis=1, concat_axis=0, tiled=True),
        lax.all_to_all(block_scales, "inner", split_axis=1, concat_axis=0, tiled=True),
        lax.all_to_all(gate_logits, "inner", split_axis=1, concat_axis=0, tiled=True),
    )
    regrouped = dequantize(coded_share, scale_share)
    token_count = regrouped.shape[0]
    previous = from_behind(regrouped[token_count - CONV + 1 :], "outer", 1)
    mixed = convolve(jnp.concatenate([previous, regrouped], axis=0), conv_weight, token_count)
    queries, keys_in, values_in, beta_gate, log_decay = split_heads(
        mixed, gate_share, decay_log, dt_bias
    )
    update_part, write_part, attend, grown_query, carried_keys, decay_total = block_terms(
        queries, keys_in, values_in, beta_gate, log_decay
    )
    head_count = queries.shape[1]
    zero_state = jnp.zeros((head_count, HD, HD), jnp.float32)
    identity = jnp.broadcast_to(jnp.eye(HD, dtype=jnp.float32), (head_count, HD, HD))
    start_pair = jnp.concatenate([zero_state, identity], axis=-1)
    sequence = (update_part, write_part, carried_keys, decay_total)
    final_pair, start_pairs = lax.scan(step_pair, start_pair, sequence, unroll=True)
    incoming = incoming_state(final_pair, "outer")
    effective_query = grown_query - jnp.einsum(
        "...ce,...ek->...ck", attend, write_part, precision=HIGH_PRECISION
    )
    local_part = jnp.einsum(
        "...ce,...ev->...cv", attend, update_part, precision=HIGH_PRECISION
    )
    through_state = jnp.einsum(
        "...ck,...kj->...cj", effective_query, start_pairs, precision=HIGH_PRECISION
    )
    local_part = local_part + through_state[..., :HD]
    outputs = local_part + jnp.einsum(
        "bhck,hkv->bhcv", through_state[..., HD:], incoming, precision=HIGH_PRECISION
    )
    scaled = (
        outputs
        * lax.rsqrt(jnp.mean(outputs * outputs, axis=-1, keepdims=True) + EPS_NORM)
        * norm_gain
    )
    normed = scaled.astype(jnp.bfloat16)
    by_token = jnp.swapaxes(normed, 1, 2).reshape(token_count, head_count, HD)
    return lax.all_to_all(by_token, "inner", split_axis=0, concat_axis=1, tiled=True)


def solution(mesh):
    placed = (
        P(("outer", "inner"), None, None),
        P(("outer", "inner"), None, None),
        P(("outer", "inner"), None, None),
        P(None, "inner", None),
        P("inner"),
        P("inner"),
        P(),
    )
    return jax.shard_map(
        local,
        mesh=mesh,
        in_specs=placed,
        out_specs=P(("outer", "inner"), None, None),
        check_vma=False,
    )
```

```python
import jax
import jax.numpy as jnp
from jax import lax
from jax.sharding import PartitionSpec as P

HD = 128
BLOCK = 128
QB = 32
CONV = 4


HIGH_PRECISION = lax.Precision.HIGHEST
FAST_PRECISION = lax.Precision.HIGH
EPS_NORM = 1e-06


def from_behind(value, axis, steps):
    count = lax.axis_size(axis)
    leading, last = (max(0, -steps), min(count, count - steps))
    return lax.ppermute(value, axis, [(source, source + steps) for source in range(leading, last)])


def dequantize(blocks, per_token):
    channels = blocks.shape[2]
    quarter = channels // 4
    per_token = per_token.astype(jnp.float32)
    group = lax.broadcasted_iota(jnp.int32, (1, 1, channels), 2) // quarter
    spread = jnp.broadcast_to(per_token[..., 0:1], blocks.shape)
    for part in range(1, 4):
        spread = jnp.where(group == part, per_token[..., part : part + 1], spread)
    return blocks.astype(jnp.float32) * spread


def convolve(extended, conv_weight, token_count):
    summed = conv_weight[0] * extended[0:token_count]
    for offset in range(1, CONV):
        summed = summed + conv_weight[offset] * extended[offset : offset + token_count]
    return jax.nn.silu(summed)


def unit_rows(matrix):
    return matrix * lax.rsqrt(jnp.sum(matrix * matrix, axis=-1, keepdims=True) + EPS_NORM)


def split_heads(mixed, gate_share, decay_log, dt_bias):
    token_count = mixed.shape[0]
    value_heads = 2 * mixed.shape[1]
    block_count = token_count // BLOCK
    queries = jnp.repeat(unit_rows(mixed[:, :, :HD]), 2, axis=1)
    keys_in = jnp.repeat(unit_rows(mixed[:, :, HD : 2 * HD]), 2, axis=1)
    values_in = mixed[:, :, 2 * HD :].reshape(token_count, value_heads, HD)
    gate_values = gate_share.astype(jnp.float32)
    beta_gate = jax.nn.sigmoid(gate_values[:, :, :2].reshape(token_count, value_heads))
    raw_decay = gate_values[:, :, 2:].reshape(token_count, value_heads)
    log_decay = -jnp.exp(decay_log) * jax.nn.softplus(raw_decay + dt_bias)

    def blocked(tensor):
        return jnp.swapaxes(tensor.reshape((block_count, BLOCK) + tensor.shape[1:]), 1, 2)

    return (
        blocked(queries),
        blocked(keys_in),
        blocked(values_in),
        blocked(beta_gate),
        blocked(log_decay),
    )


def lower_inverse(strict_part, length):
    negated = -strict_part
    eye_block = jnp.eye(length, dtype=jnp.float32)
    inverse = eye_block + negated
    power = negated
    for unused_level in range((length - 1).bit_length() - 1):
        power = jnp.einsum("...ij,...jk->...ik", power, power, precision=FAST_PRECISION)
        inverse = inverse + jnp.einsum(
            "...ij,...jk->...ik", inverse, power, precision=FAST_PRECISION
        )
    return inverse


def block_terms(queries, keys_in, values_in, beta_gate, log_decay):
    cumulative = jnp.cumsum(log_decay, axis=-1)
    length = log_decay.shape[-1]
    row_index = lax.broadcasted_iota(jnp.int32, (length, length), 0)
    col_index = lax.broadcasted_iota(jnp.int32, (length, length), 1)
    lower_mask = row_index >= col_index
    strict = row_index > col_index
    differ = cumulative[..., :, None] - cumulative[..., None, :]
    weights = jnp.where(lower_mask, jnp.exp(jnp.where(lower_mask, differ, 0.0)), 0.0)
    key_dots = jnp.einsum("...cd,...ed->...ce", keys_in, keys_in, precision=HIGH_PRECISION)
    strict_part = jnp.where(strict, key_dots * weights * beta_gate[..., :, None], 0.0)
    growth = jnp.exp(cumulative)
    right_side = jnp.concatenate(
        [beta_gate[..., None] * values_in, (beta_gate * growth)[..., None] * keys_in], axis=-1
    )
    inverse = lower_inverse(strict_part, length)
    solved = jnp.einsum("...ce,...ed->...cd", inverse, right_side, precision=HIGH_PRECISION)
    head_width = values_in.shape[-1]
    update_part = solved[..., :head_width]
    write_part = solved[..., head_width:]
    attend = jnp.einsum("...cd,...ed->...ce", queries, keys_in, precision=HIGH_PRECISION) * weights
    final_sum = cumulative[..., -1]
    carried_keys = jnp.exp(final_sum[..., None] - cumulative)[..., None] * keys_in
    return (
        update_part,
        write_part,
        attend,
        growth[..., None] * queries,
        carried_keys,
        jnp.exp(final_sum),
    )


def advance(current_state, incoming_value_rows, carried_keys, decay_total):
    return decay_total[..., None, None] * current_state + jnp.einsum(
        "...ck,...cv->...kv", carried_keys, incoming_value_rows, precision=HIGH_PRECISION
    )


def pair_update(passed_block_state, inputs):
    current_update, current_write, carried_now, decay_now = inputs
    target_values = jnp.concatenate([current_update, jnp.zeros_like(current_update)], axis=-1)
    incoming_value_rows = target_values - jnp.einsum(
        "zsg,zgj->zsj", current_write, passed_block_state, precision=HIGH_PRECISION
    )
    return advance(passed_block_state, incoming_value_rows, carried_now, decay_now)


def shifted(value, axis, steps):
    count = lax.axis_size(axis)
    return lax.ppermute(value, axis, [(source, source + steps) for source in range(count - steps)])


def incoming_state(pair, axis):
    count = lax.axis_size(axis)
    place = lax.axis_index(axis)
    state = pair[..., :HD]
    if count == 1:
        return jnp.zeros_like(state)
    width = 1
    while 2 * width < count:
        got = shifted(pair, axis, width)
        joined = jnp.einsum("hij,hjk->hik", pair[..., HD:], got, precision=HIGH_PRECISION)
        joined = joined + jnp.concatenate([pair[..., :HD], jnp.zeros_like(state)], axis=-1)
        pair = jnp.where(place >= width, joined, pair)
        width *= 2
    previous = shifted(pair, axis, 1)
    result = previous[..., :HD]
    if width + 1 < count:
        far_state = shifted(pair[..., :HD], axis, width + 1)
        result = result + jnp.einsum(
            "hij,hjk->hik", previous[..., HD:], far_state, precision=HIGH_PRECISION
        )
    return result


def step_pair(pair, inputs):
    return (pair_update(pair, inputs), pair)


def local(qkv_blocks, block_scales, gate_logits, conv_weight, decay_log, dt_bias, norm_gain):
    side = jnp.concatenate([jnp.repeat(block_scales, QB, axis=0), gate_logits], axis=-1)
    coded_share = lax.all_to_all(qkv_blocks, "inner", split_axis=1, concat_axis=0, tiled=True)
    side_share = lax.all_to_all(side, "inner", split_axis=1, concat_axis=0, tiled=True)
    gate_share = side_share[..., 4:]
    regrouped = dequantize(coded_share, side_share[..., :4])
    token_count = regrouped.shape[0]
    previous = from_behind(regrouped[token_count - CONV + 1 :], "outer", 1)
    mixed = convolve(jnp.concatenate([previous, regrouped], axis=0), conv_weight, token_count)
    queries, keys_in, values_in, beta_gate, log_decay = split_heads(
        mixed, gate_share, decay_log, dt_bias
    )
    update_part, write_part, attend, grown_query, carried_keys, decay_total = block_terms(
        queries, keys_in, values_in, beta_gate, log_decay
    )
    head_count = queries.shape[1]
    zero_state = jnp.zeros((head_count, HD, HD), jnp.float32)
    identity = jnp.broadcast_to(jnp.eye(HD, dtype=jnp.float32), (head_count, HD, HD))
    start_pair = jnp.concatenate([zero_state, identity], axis=-1)
    sequence = (update_part, write_part, carried_keys, decay_total)
    final_pair, start_pairs = lax.scan(step_pair, start_pair, sequence, unroll=True)
    incoming = incoming_state(final_pair, "outer")
    effective_query = grown_query - jnp.einsum(
        "...ce,...ek->...ck", attend, write_part, precision=HIGH_PRECISION
    )
    local_part = jnp.einsum(
        "...ce,...ev->...cv", attend, update_part, precision=HIGH_PRECISION
    )
    through_state = jnp.einsum(
        "...ck,...kj->...cj", effective_query, start_pairs, precision=HIGH_PRECISION
    )
    local_part = local_part + through_state[..., :HD]
    outputs = local_part + jnp.einsum(
        "bhck,hkv->bhcv", through_state[..., HD:], incoming, precision=HIGH_PRECISION
    )
    scaled = (
        outputs
        * lax.rsqrt(jnp.mean(outputs * outputs, axis=-1, keepdims=True) + EPS_NORM)
        * norm_gain
    )
    normed = scaled.astype(jnp.bfloat16)
    by_token = jnp.swapaxes(normed, 1, 2).reshape(token_count, head_count, HD)
    return lax.all_to_all(by_token, "inner", split_axis=0, concat_axis=1, tiled=True)


def solution(mesh):
    placed = (
        P(("outer", "inner"), None, None),
        P(("outer", "inner"), None, None),
        P(("outer", "inner"), None, None),
        P(None, "inner", None),
        P("inner"),
        P("inner"),
        P(),
    )
    return jax.shard_map(
        local,
        mesh=mesh,
        in_specs=placed,
        out_specs=P(("outer", "inner"), None, None),
        check_vma=False,
    )
```

```python
import jax
import jax.numpy as jnp
from jax import lax
from jax.sharding import PartitionSpec as P

HD = 128
BLOCK = 128
QB = 32
CONV = 4


HIGH_PRECISION = lax.Precision.HIGHEST
FAST_PRECISION = lax.Precision.HIGH
EPS_NORM = 1e-06


def from_behind(value, axis, steps):
    count = lax.axis_size(axis)
    leading, last = (max(0, -steps), min(count, count - steps))
    return lax.ppermute(value, axis, [(source, source + steps) for source in range(leading, last)])


def dequantize(blocks, per_token):
    channels = blocks.shape[2]
    groups = per_token.shape[-1]
    quarter = channels // groups
    per_token = per_token.astype(jnp.float32)
    group = lax.broadcasted_iota(jnp.int32, (1, 1, channels), 2) // quarter
    spread = jnp.broadcast_to(per_token[..., 0:1], blocks.shape)
    for part in range(1, groups):
        spread = jnp.where(group == part, per_token[..., part : part + 1], spread)
    return blocks.astype(jnp.float32) * spread


def convolve(extended, conv_weight, token_count):
    summed = conv_weight[0] * extended[0:token_count]
    for offset in range(1, CONV):
        summed = summed + conv_weight[offset] * extended[offset : offset + token_count]
    return jax.nn.silu(summed)


def unit_rows(matrix):
    return matrix * lax.rsqrt(jnp.sum(matrix * matrix, axis=-1, keepdims=True) + EPS_NORM)


def split_heads(mixed, values_in, gate_share, decay_log, dt_bias):
    token_count = mixed.shape[0]
    value_heads = 2 * mixed.shape[1]
    block_count = token_count // BLOCK
    queries = jnp.repeat(unit_rows(mixed[:, :, :HD]), 2, axis=1)
    keys_in = jnp.repeat(unit_rows(mixed[:, :, HD : 2 * HD]), 2, axis=1)
    gate_values = gate_share.astype(jnp.float32)
    beta_gate = jax.nn.sigmoid(gate_values[:, :, :2].reshape(token_count, value_heads))
    raw_decay = gate_values[:, :, 2:].reshape(token_count, value_heads)
    log_decay = -jnp.exp(decay_log) * jax.nn.softplus(raw_decay + dt_bias)

    def blocked(tensor):
        return jnp.swapaxes(tensor.reshape((block_count, BLOCK) + tensor.shape[1:]), 1, 2)

    return (
        blocked(queries),
        blocked(keys_in),
        blocked(values_in),
        blocked(beta_gate),
        blocked(log_decay),
    )


def lower_inverse(strict_part, length):
    negated = -strict_part
    eye_block = jnp.eye(length, dtype=jnp.float32)
    inverse = eye_block + negated
    power = negated
    for unused_level in range((length - 1).bit_length() - 1):
        power = jnp.einsum("...ij,...jk->...ik", power, power, precision=FAST_PRECISION)
        inverse = inverse + jnp.einsum(
            "...ij,...jk->...ik", inverse, power, precision=FAST_PRECISION
        )
    return inverse


def block_terms(queries, keys_in, values_in, beta_gate, log_decay):
    cumulative = jnp.cumsum(log_decay, axis=-1)
    length = log_decay.shape[-1]
    row_index = lax.broadcasted_iota(jnp.int32, (length, length), 0)
    col_index = lax.broadcasted_iota(jnp.int32, (length, length), 1)
    lower_mask = row_index >= col_index
    strict = row_index > col_index
    differ = cumulative[..., :, None] - cumulative[..., None, :]
    weights = jnp.where(lower_mask, jnp.exp(jnp.where(lower_mask, differ, 0.0)), 0.0)
    key_dots = jnp.einsum("...cd,...ed->...ce", keys_in, keys_in, precision=HIGH_PRECISION)
    strict_part = jnp.where(strict, key_dots * weights * beta_gate[..., :, None], 0.0)
    growth = jnp.exp(cumulative)
    right_side = jnp.concatenate(
        [beta_gate[..., None] * values_in, (beta_gate * growth)[..., None] * keys_in], axis=-1
    )
    inverse = lower_inverse(strict_part, length)
    solved = jnp.einsum("...ce,...ed->...cd", inverse, right_side, precision=HIGH_PRECISION)
    head_width = values_in.shape[-1]
    update_part = solved[..., :head_width]
    write_part = solved[..., head_width:]
    attend = jnp.einsum("...cd,...ed->...ce", queries, keys_in, precision=HIGH_PRECISION) * weights
    final_sum = cumulative[..., -1]
    carried_keys = jnp.exp(final_sum[..., None] - cumulative)[..., None] * keys_in
    return (
        update_part,
        write_part,
        attend,
        growth[..., None] * queries,
        carried_keys,
        jnp.exp(final_sum),
    )


def advance(current_state, incoming_value_rows, carried_keys, decay_total):
    return decay_total[..., None, None] * current_state + jnp.einsum(
        "...ck,...cv->...kv", carried_keys, incoming_value_rows, precision=HIGH_PRECISION
    )


def pair_update(passed_block_state, inputs):
    current_update, current_write, carried_now, decay_now = inputs
    target_values = jnp.concatenate([current_update, jnp.zeros_like(current_update)], axis=-1)
    incoming_value_rows = target_values - jnp.einsum(
        "zsg,zgj->zsj", current_write, passed_block_state, precision=HIGH_PRECISION
    )
    return advance(passed_block_state, incoming_value_rows, carried_now, decay_now)


def shifted(value, axis, steps):
    count = lax.axis_size(axis)
    return lax.ppermute(value, axis, [(source, source + steps) for source in range(count - steps)])


def incoming_state(pair, axis):
    count = lax.axis_size(axis)
    place = lax.axis_index(axis)
    state = pair[..., :HD]
    if count == 1:
        return jnp.zeros_like(state)
    width = 1
    while 2 * width < count:
        got = shifted(pair, axis, width)
        joined = jnp.einsum("hij,hjk->hik", pair[..., HD:], got, precision=HIGH_PRECISION)
        joined = joined + jnp.concatenate([pair[..., :HD], jnp.zeros_like(state)], axis=-1)
        pair = jnp.where(place >= width, joined, pair)
        width *= 2
    previous = shifted(pair, axis, 1)
    result = previous[..., :HD]
    if width + 1 < count:
        far_state = shifted(pair[..., :HD], axis, width + 1)
        result = result + jnp.einsum(
            "hij,hjk->hik", previous[..., HD:], far_state, precision=HIGH_PRECISION
        )
    return result


def step_pair(pair, inputs):
    return (pair_update(pair, inputs), pair)


def local(qkv_blocks, block_scales, gate_logits, conv_weight, decay_log, dt_bias, norm_gain):
    side = jnp.concatenate([jnp.repeat(block_scales, QB, axis=0), gate_logits], axis=-1)
    coded_share = lax.all_to_all(qkv_blocks, "inner", split_axis=1, concat_axis=0, tiled=True)
    side_share = lax.all_to_all(side, "inner", split_axis=1, concat_axis=0, tiled=True)
    gate_share = side_share[..., 4:]
    token_count, key_share, channels = coded_share.shape
    value_heads = 2 * key_share
    scale_share = side_share[..., :4]
    paired = dequantize(coded_share[:, :, : 2 * HD], scale_share[..., :2])
    value_scale = scale_share[..., 2:].reshape(token_count, value_heads, 1)
    valued = coded_share[:, :, 2 * HD :].reshape(token_count, value_heads, HD).astype(
        jnp.float32
    ) * value_scale.astype(jnp.float32)
    tail = CONV - 1
    rim = jnp.concatenate(
        [
            paired[token_count - tail :].reshape(tail, -1),
            valued[token_count - tail :].reshape(tail, -1),
        ],
        axis=1,
    )
    rim = from_behind(rim, "outer", 1)
    split_at = key_share * 2 * HD
    paired_rim = rim[:, :split_at].reshape(tail, key_share, 2 * HD)
    valued_rim = rim[:, split_at:].reshape(tail, value_heads, HD)
    mixed = convolve(
        jnp.concatenate([paired_rim, paired], axis=0), conv_weight[:, :, : 2 * HD], token_count
    )
    values_mixed = convolve(
        jnp.concatenate([valued_rim, valued], axis=0),
        conv_weight[:, :, 2 * HD :].reshape(CONV, value_heads, HD),
        token_count,
    )
    queries, keys_in, values_in, beta_gate, log_decay = split_heads(
        mixed, values_mixed, gate_share, decay_log, dt_bias
    )
    update_part, write_part, attend, grown_query, carried_keys, decay_total = block_terms(
        queries, keys_in, values_in, beta_gate, log_decay
    )
    head_count = queries.shape[1]
    zero_state = jnp.zeros((head_count, HD, HD), jnp.float32)
    identity = jnp.broadcast_to(jnp.eye(HD, dtype=jnp.float32), (head_count, HD, HD))
    start_pair = jnp.concatenate([zero_state, identity], axis=-1)
    sequence = (update_part, write_part, carried_keys, decay_total)
    final_pair, start_pairs = lax.scan(step_pair, start_pair, sequence, unroll=True)
    incoming = incoming_state(final_pair, "outer")
    effective_query = grown_query - jnp.einsum(
        "...ce,...ek->...ck", attend, write_part, precision=HIGH_PRECISION
    )
    local_part = jnp.einsum(
        "...ce,...ev->...cv", attend, update_part, precision=HIGH_PRECISION
    )
    through_state = jnp.einsum(
        "...ck,...kj->...cj", effective_query, start_pairs, precision=HIGH_PRECISION
    )
    local_part = local_part + through_state[..., :HD]
    outputs = local_part + jnp.einsum(
        "bhck,hkv->bhcv", through_state[..., HD:], incoming, precision=HIGH_PRECISION
    )
    scaled = (
        outputs
        * lax.rsqrt(jnp.mean(outputs * outputs, axis=-1, keepdims=True) + EPS_NORM)
        * norm_gain
    )
    normed = scaled.astype(jnp.bfloat16)
    by_token = jnp.swapaxes(normed, 1, 2).reshape(token_count, head_count, HD)
    return lax.all_to_all(by_token, "inner", split_axis=0, concat_axis=1, tiled=True)


def solution(mesh):
    placed = (
        P(("outer", "inner"), None, None),
        P(("outer", "inner"), None, None),
        P(("outer", "inner"), None, None),
        P(None, "inner", None),
        P("inner"),
        P("inner"),
        P(),
    )
    return jax.shard_map(
        local,
        mesh=mesh,
        in_specs=placed,
        out_specs=P(("outer", "inner"), None, None),
        check_vma=False,
    )
```

```python
import jax
import jax.numpy as jnp
from jax import lax
from jax.sharding import PartitionSpec as P

HD = 128
BLOCK = 128
QB = 32
CONV = 4


HIGH_PRECISION = lax.Precision.HIGHEST
FAST_PRECISION = lax.Precision.HIGH
EPS_NORM = 1e-06


def from_behind(value, axis, steps):
    count = lax.axis_size(axis)
    leading, last = (max(0, -steps), min(count, count - steps))
    return lax.ppermute(value, axis, [(source, source + steps) for source in range(leading, last)])


def dequantize(blocks, per_token):
    channels = blocks.shape[2]
    quarter = channels // 4
    per_token = per_token.astype(jnp.float32)
    group = lax.broadcasted_iota(jnp.int32, (1, 1, channels), 2) // quarter
    spread = jnp.broadcast_to(per_token[..., 0:1], blocks.shape)
    for part in range(1, 4):
        spread = jnp.where(group == part, per_token[..., part : part + 1], spread)
    return blocks.astype(jnp.float32) * spread


def convolve(extended, conv_weight, token_count):
    summed = conv_weight[0] * extended[0:token_count]
    for offset in range(1, CONV):
        summed = summed + conv_weight[offset] * extended[offset : offset + token_count]
    return jax.nn.silu(summed)


def unit_rows(matrix):
    return matrix * lax.rsqrt(jnp.sum(matrix * matrix, axis=-1, keepdims=True) + EPS_NORM)


def split_heads(mixed, gate_share, decay_log, dt_bias):
    token_count = mixed.shape[0]
    value_heads = 2 * mixed.shape[1]
    block_count = token_count // BLOCK
    queries = jnp.repeat(unit_rows(mixed[:, :, :HD]), 2, axis=1)
    keys_in = jnp.repeat(unit_rows(mixed[:, :, HD : 2 * HD]), 2, axis=1)
    values_in = mixed[:, :, 2 * HD :].reshape(token_count, value_heads, HD)
    gate_values = gate_share.astype(jnp.float32)
    beta_gate = jax.nn.sigmoid(gate_values[:, :, :2].reshape(token_count, value_heads))
    raw_decay = gate_values[:, :, 2:].reshape(token_count, value_heads)
    log_decay = -jnp.exp(decay_log) * jax.nn.softplus(raw_decay + dt_bias)

    def blocked(tensor):
        return jnp.swapaxes(tensor.reshape((block_count, BLOCK) + tensor.shape[1:]), 1, 2)

    return (
        blocked(queries),
        blocked(keys_in),
        blocked(values_in),
        blocked(beta_gate),
        blocked(log_decay),
    )


def lower_inverse(strict_part, length):
    negated = -strict_part
    eye_block = jnp.eye(length, dtype=jnp.float32)
    inverse = eye_block + negated
    power = negated
    for unused_level in range((length - 1).bit_length() - 1):
        power = jnp.einsum("...ij,...jk->...ik", power, power, precision=FAST_PRECISION)
        inverse = inverse + jnp.einsum(
            "...ij,...jk->...ik", inverse, power, precision=FAST_PRECISION
        )
    return inverse


def block_terms(queries, keys_in, values_in, beta_gate, log_decay):
    cumulative = jnp.cumsum(log_decay, axis=-1)
    length = log_decay.shape[-1]
    row_index = lax.broadcasted_iota(jnp.int32, (length, length), 0)
    col_index = lax.broadcasted_iota(jnp.int32, (length, length), 1)
    lower_mask = row_index >= col_index
    strict = row_index > col_index
    differ = cumulative[..., :, None] - cumulative[..., None, :]
    weights = jnp.where(lower_mask, jnp.exp(jnp.where(lower_mask, differ, 0.0)), 0.0)
    key_dots = jnp.einsum("...cd,...ed->...ce", keys_in, keys_in, precision=HIGH_PRECISION)
    strict_part = jnp.where(strict, key_dots * weights * beta_gate[..., :, None], 0.0)
    growth = jnp.exp(cumulative)
    right_side = jnp.concatenate(
        [beta_gate[..., None] * values_in, (beta_gate * growth)[..., None] * keys_in], axis=-1
    )
    inverse = lower_inverse(strict_part, length)
    solved = jnp.einsum("...ce,...ed->...cd", inverse, right_side, precision=HIGH_PRECISION)
    head_width = values_in.shape[-1]
    update_part = solved[..., :head_width]
    write_part = solved[..., head_width:]
    attend = jnp.einsum("...cd,...ed->...ce", queries, keys_in, precision=HIGH_PRECISION) * weights
    final_sum = cumulative[..., -1]
    carried_keys = jnp.exp(final_sum[..., None] - cumulative)[..., None] * keys_in
    return (
        update_part,
        write_part,
        attend,
        growth[..., None] * queries,
        carried_keys,
        jnp.exp(final_sum),
    )


def advance(current_state, incoming_value_rows, carried_keys, decay_total):
    return decay_total[..., None, None] * current_state + jnp.einsum(
        "...ck,...cv->...kv", carried_keys, incoming_value_rows, precision=HIGH_PRECISION
    )


def pair_update(passed_block_state, inputs):
    current_update, current_write, carried_now, decay_now = inputs
    target_values = jnp.concatenate([current_update, jnp.zeros_like(current_update)], axis=-1)
    incoming_value_rows = target_values - jnp.einsum(
        "zsg,zgj->zsj", current_write, passed_block_state, precision=HIGH_PRECISION
    )
    return advance(passed_block_state, incoming_value_rows, carried_now, decay_now)


def shifted(value, axis, steps):
    count = lax.axis_size(axis)
    return lax.ppermute(value, axis, [(source, source + steps) for source in range(count - steps)])


def incoming_state(pair, axis):
    count = lax.axis_size(axis)
    place = lax.axis_index(axis)
    state = pair[..., :HD]
    if count == 1:
        return jnp.zeros_like(state)
    width = 1
    while 2 * width < count:
        got = shifted(pair, axis, width)
        joined = jnp.einsum("hij,hjk->hik", pair[..., HD:], got, precision=FAST_PRECISION)
        joined = joined + jnp.concatenate([pair[..., :HD], jnp.zeros_like(state)], axis=-1)
        pair = jnp.where(place >= width, joined, pair)
        width *= 2
    previous = shifted(pair, axis, 1)
    result = previous[..., :HD]
    if width + 1 < count:
        far_state = shifted(pair[..., :HD], axis, width + 1)
        result = result + jnp.einsum(
            "hij,hjk->hik", previous[..., HD:], far_state, precision=FAST_PRECISION
        )
    return result


def step_pair(pair, inputs):
    return (pair_update(pair, inputs), pair)


def local(qkv_blocks, block_scales, gate_logits, conv_weight, decay_log, dt_bias, norm_gain):
    side = jnp.concatenate([jnp.repeat(block_scales, QB, axis=0), gate_logits], axis=-1)
    coded_share = lax.all_to_all(qkv_blocks, "inner", split_axis=1, concat_axis=0, tiled=True)
    side_share = lax.all_to_all(side, "inner", split_axis=1, concat_axis=0, tiled=True)
    gate_share = side_share[..., 4:]
    regrouped = dequantize(coded_share, side_share[..., :4])
    token_count = regrouped.shape[0]
    previous = from_behind(regrouped[token_count - CONV + 1 :], "outer", 1)
    mixed = convolve(jnp.concatenate([previous, regrouped], axis=0), conv_weight, token_count)
    queries, keys_in, values_in, beta_gate, log_decay = split_heads(
        mixed, gate_share, decay_log, dt_bias
    )
    update_part, write_part, attend, grown_query, carried_keys, decay_total = block_terms(
        queries, keys_in, values_in, beta_gate, log_decay
    )
    head_count = queries.shape[1]
    zero_state = jnp.zeros((head_count, HD, HD), jnp.float32)
    identity = jnp.broadcast_to(jnp.eye(HD, dtype=jnp.float32), (head_count, HD, HD))
    start_pair = jnp.concatenate([zero_state, identity], axis=-1)
    sequence = (update_part, write_part, carried_keys, decay_total)
    final_pair, start_pairs = lax.scan(step_pair, start_pair, sequence, unroll=True)
    incoming = incoming_state(final_pair, "outer")
    effective_query = grown_query - jnp.einsum(
        "...ce,...ek->...ck", attend, write_part, precision=HIGH_PRECISION
    )
    local_part = jnp.einsum(
        "...ce,...ev->...cv", attend, update_part, precision=HIGH_PRECISION
    )
    through_state = jnp.einsum(
        "...ck,...kj->...cj", effective_query, start_pairs, precision=HIGH_PRECISION
    )
    local_part = local_part + through_state[..., :HD]
    outputs = local_part + jnp.einsum(
        "bhck,hkv->bhcv", through_state[..., HD:], incoming, precision=HIGH_PRECISION
    )
    scaled = (
        outputs
        * lax.rsqrt(jnp.mean(outputs * outputs, axis=-1, keepdims=True) + EPS_NORM)
        * norm_gain
    )
    normed = scaled.astype(jnp.bfloat16)
    by_token = jnp.swapaxes(normed, 1, 2).reshape(token_count, head_count, HD)
    return lax.all_to_all(by_token, "inner", split_axis=0, concat_axis=1, tiled=True)


def solution(mesh):
    placed = (
        P(("outer", "inner"), None, None),
        P(("outer", "inner"), None, None),
        P(("outer", "inner"), None, None),
        P(None, "inner", None),
        P("inner"),
        P("inner"),
        P(),
    )
    return jax.shard_map(
        local,
        mesh=mesh,
        in_specs=placed,
        out_specs=P(("outer", "inner"), None, None),
        check_vma=False,
    )
```

```python
import jax
import jax.numpy as jnp
from jax import lax
from jax.sharding import PartitionSpec as P

HD = 128
BLOCK = 128
QB = 32
CONV = 4


HIGH_PRECISION = lax.Precision.HIGHEST
FAST_PRECISION = lax.Precision.HIGH
EPS_NORM = 1e-06


def from_behind(value, axis, steps):
    count = lax.axis_size(axis)
    leading, last = (max(0, -steps), min(count, count - steps))
    return lax.ppermute(value, axis, [(source, source + steps) for source in range(leading, last)])


def dequantize(blocks, per_token):
    channels = blocks.shape[2]
    quarter = channels // 4
    per_token = per_token.astype(jnp.float32)
    group = lax.broadcasted_iota(jnp.int32, (1, 1, channels), 2) // quarter
    spread = jnp.broadcast_to(per_token[..., 0:1], blocks.shape)
    for part in range(1, 4):
        spread = jnp.where(group == part, per_token[..., part : part + 1], spread)
    return blocks.astype(jnp.float32) * spread


def convolve(extended, conv_weight, token_count):
    summed = conv_weight[0] * extended[0:token_count]
    for offset in range(1, CONV):
        summed = summed + conv_weight[offset] * extended[offset : offset + token_count]
    return jax.nn.silu(summed)


def unit_rows(matrix):
    return matrix * lax.rsqrt(jnp.sum(matrix * matrix, axis=-1, keepdims=True) + EPS_NORM)


def split_heads(mixed, gate_share, decay_log, dt_bias):
    token_count = mixed.shape[0]
    value_heads = 2 * mixed.shape[1]
    block_count = token_count // BLOCK
    queries = jnp.repeat(unit_rows(mixed[:, :, :HD]), 2, axis=1)
    keys_in = jnp.repeat(unit_rows(mixed[:, :, HD : 2 * HD]), 2, axis=1)
    values_in = mixed[:, :, 2 * HD :].reshape(token_count, value_heads, HD)
    gate_values = gate_share.astype(jnp.float32)
    beta_gate = jax.nn.sigmoid(gate_values[:, :, :2].reshape(token_count, value_heads))
    raw_decay = gate_values[:, :, 2:].reshape(token_count, value_heads)
    log_decay = -jnp.exp(decay_log) * jax.nn.softplus(raw_decay + dt_bias)

    def blocked(tensor):
        return jnp.swapaxes(tensor.reshape((block_count, BLOCK) + tensor.shape[1:]), 1, 2)

    return (
        blocked(queries),
        blocked(keys_in),
        blocked(values_in),
        blocked(beta_gate),
        blocked(log_decay),
    )


def lower_inverse(strict_part, length):
    negated = -strict_part
    eye_block = jnp.eye(length, dtype=jnp.float32)
    inverse = eye_block + negated
    power = negated
    for unused_level in range((length - 1).bit_length() - 1):
        power = jnp.einsum("...ij,...jk->...ik", power, power, precision=FAST_PRECISION)
        inverse = inverse + jnp.einsum(
            "...ij,...jk->...ik", inverse, power, precision=FAST_PRECISION
        )
    return inverse


def block_terms(queries, keys_in, values_in, beta_gate, log_decay):
    cumulative = jnp.cumsum(log_decay, axis=-1)
    length = log_decay.shape[-1]
    row_index = lax.broadcasted_iota(jnp.int32, (length, length), 0)
    col_index = lax.broadcasted_iota(jnp.int32, (length, length), 1)
    lower_mask = row_index >= col_index
    strict = row_index > col_index
    differ = cumulative[..., :, None] - cumulative[..., None, :]
    weights = jnp.where(lower_mask, jnp.exp(jnp.where(lower_mask, differ, 0.0)), 0.0)
    key_dots = jnp.einsum("...cd,...ed->...ce", keys_in, keys_in, precision=HIGH_PRECISION)
    strict_part = jnp.where(strict, key_dots * weights * beta_gate[..., :, None], 0.0)
    growth = jnp.exp(cumulative)
    right_side = jnp.concatenate(
        [beta_gate[..., None] * values_in, (beta_gate * growth)[..., None] * keys_in], axis=-1
    )
    inverse = lower_inverse(strict_part, length)
    solved = jnp.einsum("...ce,...ed->...cd", inverse, right_side, precision=HIGH_PRECISION)
    head_width = values_in.shape[-1]
    update_part = solved[..., :head_width]
    write_part = solved[..., head_width:]
    attend = jnp.einsum("...cd,...ed->...ce", queries, keys_in, precision=HIGH_PRECISION) * weights
    final_sum = cumulative[..., -1]
    carried_keys = jnp.exp(final_sum[..., None] - cumulative)[..., None] * keys_in
    return (
        update_part,
        write_part,
        attend,
        growth[..., None] * queries,
        carried_keys,
        jnp.exp(final_sum),
    )


def advance(current_state, incoming_value_rows, carried_keys, decay_total):
    return decay_total[..., None, None] * current_state + jnp.einsum(
        "...ck,...cv->...kv", carried_keys, incoming_value_rows, precision=HIGH_PRECISION
    )


def pair_update(passed_block_state, inputs):
    current_update, current_write, carried_now, decay_now = inputs
    target_values = jnp.concatenate([current_update, jnp.zeros_like(current_update)], axis=-1)
    incoming_value_rows = target_values - jnp.einsum(
        "zsg,zgj->zsj", current_write, passed_block_state, precision=HIGH_PRECISION
    )
    return advance(passed_block_state, incoming_value_rows, carried_now, decay_now)


def shifted(value, axis, steps):
    count = lax.axis_size(axis)
    return lax.ppermute(value, axis, [(source, source + steps) for source in range(count - steps)])


def incoming_state(pair, axis):
    count = lax.axis_size(axis)
    place = lax.axis_index(axis)
    state = pair[..., :HD]
    if count == 1:
        return jnp.zeros_like(state)
    width = 1
    while 2 * width < count:
        got = shifted(pair, axis, width)
        joined = jnp.einsum("hij,hjk->hik", pair[..., HD:], got, precision=FAST_PRECISION)
        joined = joined + jnp.concatenate([pair[..., :HD], jnp.zeros_like(state)], axis=-1)
        pair = jnp.where(place >= width, joined, pair)
        width *= 2
    previous = shifted(pair, axis, 1)
    result = previous[..., :HD]
    if width + 1 < count:
        far_state = shifted(pair[..., :HD], axis, width + 1)
        result = result + jnp.einsum(
            "hij,hjk->hik", previous[..., HD:], far_state, precision=FAST_PRECISION
        )
    return result


def step_pair(pair, inputs):
    return (pair_update(pair, inputs), pair)


def local(qkv_blocks, block_scales, gate_logits, conv_weight, decay_log, dt_bias, norm_gain):
    side = jnp.concatenate([jnp.repeat(block_scales, QB, axis=0), gate_logits], axis=-1)
    coded_share = lax.all_to_all(qkv_blocks, "inner", split_axis=1, concat_axis=0, tiled=True)
    side_share = lax.all_to_all(side, "inner", split_axis=1, concat_axis=0, tiled=True)
    gate_share = side_share[..., 4:]
    regrouped = dequantize(coded_share, side_share[..., :4])
    token_count = regrouped.shape[0]
    tail = CONV - 1
    previous = from_behind(regrouped[token_count - tail :], "outer", 1)
    body = convolve(regrouped, conv_weight, token_count - tail)
    head = convolve(jnp.concatenate([previous, regrouped[:tail]], axis=0), conv_weight, tail)
    mixed = jnp.concatenate([head, body], axis=0)
    queries, keys_in, values_in, beta_gate, log_decay = split_heads(
        mixed, gate_share, decay_log, dt_bias
    )
    update_part, write_part, attend, grown_query, carried_keys, decay_total = block_terms(
        queries, keys_in, values_in, beta_gate, log_decay
    )
    head_count = queries.shape[1]
    zero_state = jnp.zeros((head_count, HD, HD), jnp.float32)
    identity = jnp.broadcast_to(jnp.eye(HD, dtype=jnp.float32), (head_count, HD, HD))
    start_pair = jnp.concatenate([zero_state, identity], axis=-1)
    sequence = (update_part, write_part, carried_keys, decay_total)
    final_pair, start_pairs = lax.scan(step_pair, start_pair, sequence, unroll=True)
    incoming = incoming_state(final_pair, "outer")
    effective_query = grown_query - jnp.einsum(
        "...ce,...ek->...ck", attend, write_part, precision=HIGH_PRECISION
    )
    local_part = jnp.einsum(
        "...ce,...ev->...cv", attend, update_part, precision=HIGH_PRECISION
    )
    through_state = jnp.einsum(
        "...ck,...kj->...cj", effective_query, start_pairs, precision=HIGH_PRECISION
    )
    local_part = local_part + through_state[..., :HD]
    outputs = local_part + jnp.einsum(
        "bhck,hkv->bhcv", through_state[..., HD:], incoming, precision=HIGH_PRECISION
    )
    scaled = (
        outputs
        * lax.rsqrt(jnp.mean(outputs * outputs, axis=-1, keepdims=True) + EPS_NORM)
        * norm_gain
    )
    normed = scaled.astype(jnp.bfloat16)
    by_token = jnp.swapaxes(normed, 1, 2).reshape(token_count, head_count, HD)
    return lax.all_to_all(by_token, "inner", split_axis=0, concat_axis=1, tiled=True)


def solution(mesh):
    placed = (
        P(("outer", "inner"), None, None),
        P(("outer", "inner"), None, None),
        P(("outer", "inner"), None, None),
        P(None, "inner", None),
        P("inner"),
        P("inner"),
        P(),
    )
    return jax.shard_map(
        local,
        mesh=mesh,
        in_specs=placed,
        out_specs=P(("outer", "inner"), None, None),
        check_vma=False,
    )
```

```python
import jax
import jax.numpy as jnp
from jax import lax
from jax.sharding import PartitionSpec as P

HD = 128
BLOCK = 128
QB = 32
CONV = 4


HIGH_PRECISION = lax.Precision.HIGHEST
FAST_PRECISION = lax.Precision.HIGH
EPS_NORM = 1e-06


def from_behind(value, axis, steps):
    count = lax.axis_size(axis)
    leading, last = (max(0, -steps), min(count, count - steps))
    return lax.ppermute(value, axis, [(source, source + steps) for source in range(leading, last)])


def dequantize(blocks, per_token):
    channels = blocks.shape[2]
    quarter = channels // 4
    per_token = per_token.astype(jnp.float32)
    group = lax.broadcasted_iota(jnp.int32, (1, 1, channels), 2) // quarter
    spread = jnp.broadcast_to(per_token[..., 0:1], blocks.shape)
    for part in range(1, 4):
        spread = jnp.where(group == part, per_token[..., part : part + 1], spread)
    return blocks.astype(jnp.float32) * spread


def convolve(extended, conv_weight, token_count):
    summed = conv_weight[0] * extended[0:token_count]
    for offset in range(1, CONV):
        summed = summed + conv_weight[offset] * extended[offset : offset + token_count]
    return jax.nn.silu(summed)


def unit_rows(matrix):
    return matrix * lax.rsqrt(jnp.sum(matrix * matrix, axis=-1, keepdims=True) + EPS_NORM)


def split_heads(mixed, gate_share, decay_log, dt_bias):
    token_count = mixed.shape[0]
    value_heads = 2 * mixed.shape[1]
    block_count = token_count // BLOCK
    queries = jnp.repeat(unit_rows(mixed[:, :, :HD]), 2, axis=1)
    keys_in = jnp.repeat(unit_rows(mixed[:, :, HD : 2 * HD]), 2, axis=1)
    values_in = mixed[:, :, 2 * HD :].reshape(token_count, value_heads, HD)
    gate_values = gate_share.astype(jnp.float32)
    beta_gate = jax.nn.sigmoid(gate_values[:, :, :2].reshape(token_count, value_heads))
    raw_decay = gate_values[:, :, 2:].reshape(token_count, value_heads)
    log_decay = -jnp.exp(decay_log) * jax.nn.softplus(raw_decay + dt_bias)

    def blocked(tensor):
        return jnp.swapaxes(tensor.reshape((block_count, BLOCK) + tensor.shape[1:]), 1, 2)

    return (
        blocked(queries),
        blocked(keys_in),
        blocked(values_in),
        blocked(beta_gate),
        blocked(log_decay),
    )


def lower_inverse(strict_part, length):
    negated = -strict_part
    eye_block = jnp.eye(length, dtype=jnp.float32)
    inverse = eye_block + negated
    power = negated
    for unused_level in range((length - 1).bit_length() - 1):
        power = jnp.einsum("...ij,...jk->...ik", power, power, precision=FAST_PRECISION)
        inverse = inverse + jnp.einsum(
            "...ij,...jk->...ik", inverse, power, precision=FAST_PRECISION
        )
    return inverse


def block_terms(queries, keys_in, values_in, beta_gate, log_decay):
    cumulative = jnp.cumsum(log_decay, axis=-1)
    length = log_decay.shape[-1]
    row_index = lax.broadcasted_iota(jnp.int32, (length, length), 0)
    col_index = lax.broadcasted_iota(jnp.int32, (length, length), 1)
    lower_mask = row_index >= col_index
    strict = row_index > col_index
    differ = cumulative[..., :, None] - cumulative[..., None, :]
    weights = jnp.where(lower_mask, jnp.exp(jnp.where(lower_mask, differ, 0.0)), 0.0)
    weights, cumulative = lax.optimization_barrier((weights, cumulative))
    key_dots = jnp.einsum("...cd,...ed->...ce", keys_in, keys_in, precision=HIGH_PRECISION)
    strict_part = jnp.where(strict, key_dots * weights * beta_gate[..., :, None], 0.0)
    growth = jnp.exp(cumulative)
    right_side = jnp.concatenate(
        [beta_gate[..., None] * values_in, (beta_gate * growth)[..., None] * keys_in], axis=-1
    )
    inverse = lower_inverse(strict_part, length)
    solved = jnp.einsum("...ce,...ed->...cd", inverse, right_side, precision=HIGH_PRECISION)
    head_width = values_in.shape[-1]
    update_part = solved[..., :head_width]
    write_part = solved[..., head_width:]
    attend = jnp.einsum("...cd,...ed->...ce", queries, keys_in, precision=HIGH_PRECISION) * weights
    final_sum = cumulative[..., -1]
    carried_keys = jnp.exp(final_sum[..., None] - cumulative)[..., None] * keys_in
    return (
        update_part,
        write_part,
        attend,
        growth[..., None] * queries,
        carried_keys,
        jnp.exp(final_sum),
    )


def advance(current_state, incoming_value_rows, carried_keys, decay_total):
    return decay_total[..., None, None] * current_state + jnp.einsum(
        "...ck,...cv->...kv", carried_keys, incoming_value_rows, precision=HIGH_PRECISION
    )


def pair_update(passed_block_state, inputs):
    current_update, current_write, carried_now, decay_now = inputs
    target_values = jnp.concatenate([current_update, jnp.zeros_like(current_update)], axis=-1)
    incoming_value_rows = target_values - jnp.einsum(
        "zsg,zgj->zsj", current_write, passed_block_state, precision=HIGH_PRECISION
    )
    return advance(passed_block_state, incoming_value_rows, carried_now, decay_now)


def shifted(value, axis, steps):
    count = lax.axis_size(axis)
    return lax.ppermute(value, axis, [(source, source + steps) for source in range(count - steps)])


def incoming_state(pair, axis):
    count = lax.axis_size(axis)
    place = lax.axis_index(axis)
    state = pair[..., :HD]
    if count == 1:
        return jnp.zeros_like(state)
    width = 1
    while 2 * width < count:
        got = shifted(pair, axis, width)
        joined = jnp.einsum("hij,hjk->hik", pair[..., HD:], got, precision=FAST_PRECISION)
        joined = joined + jnp.concatenate([pair[..., :HD], jnp.zeros_like(state)], axis=-1)
        pair = jnp.where(place >= width, joined, pair)
        width *= 2
    previous = shifted(pair, axis, 1)
    result = previous[..., :HD]
    if width + 1 < count:
        far_state = shifted(pair[..., :HD], axis, width + 1)
        result = result + jnp.einsum(
            "hij,hjk->hik", previous[..., HD:], far_state, precision=FAST_PRECISION
        )
    return result


def step_pair(pair, inputs):
    return (pair_update(pair, inputs), pair)


def local(qkv_blocks, block_scales, gate_logits, conv_weight, decay_log, dt_bias, norm_gain):
    side = jnp.concatenate([jnp.repeat(block_scales, QB, axis=0), gate_logits], axis=-1)
    coded_share = lax.all_to_all(qkv_blocks, "inner", split_axis=1, concat_axis=0, tiled=True)
    side_share = lax.all_to_all(side, "inner", split_axis=1, concat_axis=0, tiled=True)
    gate_share = side_share[..., 4:]
    regrouped = dequantize(coded_share, side_share[..., :4])
    token_count = regrouped.shape[0]
    tail = CONV - 1
    previous = from_behind(regrouped[token_count - tail :], "outer", 1)
    body = convolve(regrouped, conv_weight, token_count - tail)
    head = convolve(jnp.concatenate([previous, regrouped[:tail]], axis=0), conv_weight, tail)
    mixed = jnp.concatenate([head, body], axis=0)
    queries, keys_in, values_in, beta_gate, log_decay = split_heads(
        mixed, gate_share, decay_log, dt_bias
    )
    update_part, write_part, attend, grown_query, carried_keys, decay_total = block_terms(
        queries, keys_in, values_in, beta_gate, log_decay
    )
    head_count = queries.shape[1]
    zero_state = jnp.zeros((head_count, HD, HD), jnp.float32)
    identity = jnp.broadcast_to(jnp.eye(HD, dtype=jnp.float32), (head_count, HD, HD))
    start_pair = jnp.concatenate([zero_state, identity], axis=-1)
    sequence = (update_part, write_part, carried_keys, decay_total)
    final_pair, start_pairs = lax.scan(step_pair, start_pair, sequence, unroll=True)
    incoming = incoming_state(final_pair, "outer")
    effective_query = grown_query - jnp.einsum(
        "...ce,...ek->...ck", attend, write_part, precision=HIGH_PRECISION
    )
    local_part = jnp.einsum(
        "...ce,...ev->...cv", attend, update_part, precision=HIGH_PRECISION
    )
    through_state = jnp.einsum(
        "...ck,...kj->...cj", effective_query, start_pairs, precision=HIGH_PRECISION
    )
    local_part = local_part + through_state[..., :HD]
    outputs = local_part + jnp.einsum(
        "bhck,hkv->bhcv", through_state[..., HD:], incoming, precision=HIGH_PRECISION
    )
    scaled = (
        outputs
        * lax.rsqrt(jnp.mean(outputs * outputs, axis=-1, keepdims=True) + EPS_NORM)
        * norm_gain
    )
    normed = scaled.astype(jnp.bfloat16)
    by_token = jnp.swapaxes(normed, 1, 2).reshape(token_count, head_count, HD)
    return lax.all_to_all(by_token, "inner", split_axis=0, concat_axis=1, tiled=True)


def solution(mesh):
    placed = (
        P(("outer", "inner"), None, None),
        P(("outer", "inner"), None, None),
        P(("outer", "inner"), None, None),
        P(None, "inner", None),
        P("inner"),
        P("inner"),
        P(),
    )
    return jax.shard_map(
        local,
        mesh=mesh,
        in_specs=placed,
        out_specs=P(("outer", "inner"), None, None),
        check_vma=False,
    )
```

```python
import jax
import jax.numpy as jnp
from jax import lax
from jax.sharding import PartitionSpec as P

HD = 128
BLOCK = 128
QB = 32
CONV = 4


HIGH_PRECISION = lax.Precision.HIGHEST
FAST_PRECISION = lax.Precision.HIGH
EPS_NORM = 1e-06


def from_behind(value, axis, steps):
    count = lax.axis_size(axis)
    leading, last = (max(0, -steps), min(count, count - steps))
    return lax.ppermute(value, axis, [(source, source + steps) for source in range(leading, last)])


def dequantize(blocks, per_token):
    channels = blocks.shape[2]
    quarter = channels // 4
    per_token = per_token.astype(jnp.float32)
    group = lax.broadcasted_iota(jnp.int32, (1, 1, channels), 2) // quarter
    spread = jnp.broadcast_to(per_token[..., 0:1], blocks.shape)
    for part in range(1, 4):
        spread = jnp.where(group == part, per_token[..., part : part + 1], spread)
    return blocks.astype(jnp.float32) * spread


def convolve(extended, conv_weight, token_count):
    summed = conv_weight[0] * extended[0:token_count]
    for offset in range(1, CONV):
        summed = summed + conv_weight[offset] * extended[offset : offset + token_count]
    return jax.nn.silu(summed)


def unit_rows(matrix):
    return matrix * lax.rsqrt(jnp.sum(matrix * matrix, axis=-1, keepdims=True) + EPS_NORM)


def split_heads(mixed, gate_share, decay_log, dt_bias):
    token_count = mixed.shape[0]
    value_heads = 2 * mixed.shape[1]
    block_count = token_count // BLOCK
    queries = jnp.repeat(unit_rows(mixed[:, :, :HD]), 2, axis=1)
    keys_in = jnp.repeat(unit_rows(mixed[:, :, HD : 2 * HD]), 2, axis=1)
    values_in = mixed[:, :, 2 * HD :].reshape(token_count, value_heads, HD)
    gate_values = gate_share.astype(jnp.float32)
    beta_gate = jax.nn.sigmoid(gate_values[:, :, :2].reshape(token_count, value_heads))
    raw_decay = gate_values[:, :, 2:].reshape(token_count, value_heads)
    log_decay = -jnp.exp(decay_log) * jax.nn.softplus(raw_decay + dt_bias)

    def blocked(tensor):
        return jnp.swapaxes(tensor.reshape((block_count, BLOCK) + tensor.shape[1:]), 1, 2)

    return (
        blocked(queries),
        blocked(keys_in),
        blocked(values_in),
        blocked(beta_gate),
        blocked(log_decay),
    )


def lower_inverse(strict_part, length):
    negated = -strict_part
    eye_block = jnp.eye(length, dtype=jnp.float32)
    inverse = eye_block + negated
    power = negated
    for unused_level in range((length - 1).bit_length() - 1):
        power = jnp.einsum("...ij,...jk->...ik", power, power, precision=FAST_PRECISION)
        inverse = inverse + jnp.einsum(
            "...ij,...jk->...ik", inverse, power, precision=FAST_PRECISION
        )
    return inverse


def block_terms(queries, keys_in, values_in, beta_gate, log_decay):
    cumulative = jnp.cumsum(log_decay, axis=-1)
    length = log_decay.shape[-1]
    row_index = lax.broadcasted_iota(jnp.int32, (length, length), 0)
    col_index = lax.broadcasted_iota(jnp.int32, (length, length), 1)
    lower_mask = row_index >= col_index
    strict = row_index > col_index
    differ = cumulative[..., :, None] - cumulative[..., None, :]
    weights = jnp.where(lower_mask, jnp.exp(jnp.where(lower_mask, differ, 0.0)), 0.0)
    solve_weights = jnp.where(strict, weights * beta_gate[..., :, None], 0.0)
    weights, solve_weights, cumulative = lax.optimization_barrier(
        (weights, solve_weights, cumulative)
    )
    key_dots = jnp.einsum("...cd,...ed->...ce", keys_in, keys_in, precision=HIGH_PRECISION)
    strict_part = key_dots * solve_weights
    growth = jnp.exp(cumulative)
    right_side = jnp.concatenate(
        [beta_gate[..., None] * values_in, (beta_gate * growth)[..., None] * keys_in], axis=-1
    )
    inverse = lower_inverse(strict_part, length)
    solved = jnp.einsum("...ce,...ed->...cd", inverse, right_side, precision=HIGH_PRECISION)
    head_width = values_in.shape[-1]
    update_part = solved[..., :head_width]
    write_part = solved[..., head_width:]
    attend = jnp.einsum("...cd,...ed->...ce", queries, keys_in, precision=HIGH_PRECISION) * weights
    final_sum = cumulative[..., -1]
    carried_keys = jnp.exp(final_sum[..., None] - cumulative)[..., None] * keys_in
    return (
        update_part,
        write_part,
        attend,
        growth[..., None] * queries,
        carried_keys,
        jnp.exp(final_sum),
    )


def advance(current_state, incoming_value_rows, carried_keys, decay_total):
    return decay_total[..., None, None] * current_state + jnp.einsum(
        "...ck,...cv->...kv", carried_keys, incoming_value_rows, precision=HIGH_PRECISION
    )


def pair_update(passed_block_state, inputs):
    current_update, current_write, carried_now, decay_now = inputs
    target_values = jnp.concatenate([current_update, jnp.zeros_like(current_update)], axis=-1)
    incoming_value_rows = target_values - jnp.einsum(
        "zsg,zgj->zsj", current_write, passed_block_state, precision=HIGH_PRECISION
    )
    return advance(passed_block_state, incoming_value_rows, carried_now, decay_now)


def shifted(value, axis, steps):
    count = lax.axis_size(axis)
    return lax.ppermute(value, axis, [(source, source + steps) for source in range(count - steps)])


def incoming_state(pair, axis):
    count = lax.axis_size(axis)
    place = lax.axis_index(axis)
    state = pair[..., :HD]
    if count == 1:
        return jnp.zeros_like(state)
    width = 1
    while 2 * width < count:
        got = shifted(pair, axis, width)
        joined = jnp.einsum("hij,hjk->hik", pair[..., HD:], got, precision=FAST_PRECISION)
        joined = joined + jnp.concatenate([pair[..., :HD], jnp.zeros_like(state)], axis=-1)
        pair = jnp.where(place >= width, joined, pair)
        width *= 2
    previous = shifted(pair, axis, 1)
    result = previous[..., :HD]
    if width + 1 < count:
        far_state = shifted(pair[..., :HD], axis, width + 1)
        result = result + jnp.einsum(
            "hij,hjk->hik", previous[..., HD:], far_state, precision=FAST_PRECISION
        )
    return result


def step_pair(pair, inputs):
    return (pair_update(pair, inputs), pair)


def local(qkv_blocks, block_scales, gate_logits, conv_weight, decay_log, dt_bias, norm_gain):
    side = jnp.concatenate([jnp.repeat(block_scales, QB, axis=0), gate_logits], axis=-1)
    coded_share = lax.all_to_all(qkv_blocks, "inner", split_axis=1, concat_axis=0, tiled=True)
    side_share = lax.all_to_all(side, "inner", split_axis=1, concat_axis=0, tiled=True)
    gate_share = side_share[..., 4:]
    regrouped = dequantize(coded_share, side_share[..., :4])
    token_count = regrouped.shape[0]
    tail = CONV - 1
    previous = from_behind(regrouped[token_count - tail :], "outer", 1)
    body = convolve(regrouped, conv_weight, token_count - tail)
    head = convolve(jnp.concatenate([previous, regrouped[:tail]], axis=0), conv_weight, tail)
    mixed = jnp.concatenate([head, body], axis=0)
    queries, keys_in, values_in, beta_gate, log_decay = split_heads(
        mixed, gate_share, decay_log, dt_bias
    )
    update_part, write_part, attend, grown_query, carried_keys, decay_total = block_terms(
        queries, keys_in, values_in, beta_gate, log_decay
    )
    head_count = queries.shape[1]
    zero_state = jnp.zeros((head_count, HD, HD), jnp.float32)
    identity = jnp.broadcast_to(jnp.eye(HD, dtype=jnp.float32), (head_count, HD, HD))
    start_pair = jnp.concatenate([zero_state, identity], axis=-1)
    sequence = (update_part, write_part, carried_keys, decay_total)
    final_pair, start_pairs = lax.scan(step_pair, start_pair, sequence, unroll=True)
    incoming = incoming_state(final_pair, "outer")
    effective_query = grown_query - jnp.einsum(
        "...ce,...ek->...ck", attend, write_part, precision=HIGH_PRECISION
    )
    local_part = jnp.einsum(
        "...ce,...ev->...cv", attend, update_part, precision=HIGH_PRECISION
    )
    through_state = jnp.einsum(
        "...ck,...kj->...cj", effective_query, start_pairs, precision=HIGH_PRECISION
    )
    local_part = local_part + through_state[..., :HD]
    outputs = local_part + jnp.einsum(
        "bhck,hkv->bhcv", through_state[..., HD:], incoming, precision=HIGH_PRECISION
    )
    scaled = (
        outputs
        * lax.rsqrt(jnp.mean(outputs * outputs, axis=-1, keepdims=True) + EPS_NORM)
        * norm_gain
    )
    normed = scaled.astype(jnp.bfloat16)
    by_token = jnp.swapaxes(normed, 1, 2).reshape(token_count, head_count, HD)
    return lax.all_to_all(by_token, "inner", split_axis=0, concat_axis=1, tiled=True)


def solution(mesh):
    placed = (
        P(("outer", "inner"), None, None),
        P(("outer", "inner"), None, None),
        P(("outer", "inner"), None, None),
        P(None, "inner", None),
        P("inner"),
        P("inner"),
        P(),
    )
    return jax.shard_map(
        local,
        mesh=mesh,
        in_specs=placed,
        out_specs=P(("outer", "inner"), None, None),
        check_vma=False,
    )
```

```python
import jax
import jax.numpy as jnp
from jax import lax
from jax.sharding import PartitionSpec as P

HD = 128
BLOCK = 128
QB = 32
CONV = 4


HIGH_PRECISION = lax.Precision.HIGHEST
FAST_PRECISION = lax.Precision.HIGH
EPS_NORM = 1e-06


def from_behind(value, axis, steps):
    count = lax.axis_size(axis)
    leading, last = (max(0, -steps), min(count, count - steps))
    return lax.ppermute(value, axis, [(source, source + steps) for source in range(leading, last)])


def dequantize(blocks, per_token):
    channels = blocks.shape[2]
    quarter = channels // 4
    per_token = per_token.astype(jnp.float32)
    group = lax.broadcasted_iota(jnp.int32, (1, 1, channels), 2) // quarter
    spread = jnp.broadcast_to(per_token[..., 0:1], blocks.shape)
    for part in range(1, 4):
        spread = jnp.where(group == part, per_token[..., part : part + 1], spread)
    return blocks.astype(jnp.float32) * spread


def convolve(extended, conv_weight, token_count):
    summed = conv_weight[0] * extended[0:token_count]
    for offset in range(1, CONV):
        summed = summed + conv_weight[offset] * extended[offset : offset + token_count]
    return jax.nn.silu(summed)


def unit_rows(matrix):
    return matrix * lax.rsqrt(jnp.sum(matrix * matrix, axis=-1, keepdims=True) + EPS_NORM)


def split_heads(mixed, gate_share, decay_log, dt_bias):
    token_count = mixed.shape[0]
    value_heads = 2 * mixed.shape[1]
    block_count = token_count // BLOCK
    queries = jnp.repeat(unit_rows(mixed[:, :, :HD]), 2, axis=1)
    keys_in = jnp.repeat(unit_rows(mixed[:, :, HD : 2 * HD]), 2, axis=1)
    values_in = mixed[:, :, 2 * HD :].reshape(token_count, value_heads, HD)
    gate_values = gate_share.astype(jnp.float32)
    beta_gate = jax.nn.sigmoid(gate_values[:, :, :2].reshape(token_count, value_heads))
    raw_decay = gate_values[:, :, 2:].reshape(token_count, value_heads)
    log_decay = -jnp.exp(decay_log) * jax.nn.softplus(raw_decay + dt_bias)

    def blocked(tensor):
        return jnp.swapaxes(tensor.reshape((block_count, BLOCK) + tensor.shape[1:]), 1, 2)

    return (
        blocked(queries),
        blocked(keys_in),
        blocked(values_in),
        blocked(beta_gate),
        blocked(log_decay),
    )


def lower_inverse(strict_part, length):
    negated = -strict_part
    eye_block = jnp.eye(length, dtype=jnp.float32)
    inverse = eye_block + negated
    power = negated
    for unused_level in range((length - 1).bit_length() - 1):
        power = jnp.einsum("...ij,...jk->...ik", power, power, precision=FAST_PRECISION)
        inverse = inverse + jnp.einsum(
            "...ij,...jk->...ik", inverse, power, precision=FAST_PRECISION
        )
    return inverse


def block_terms(queries, keys_in, values_in, beta_gate, log_decay):
    cumulative = jnp.cumsum(log_decay, axis=-1)
    length = log_decay.shape[-1]
    row_index = lax.broadcasted_iota(jnp.int32, (length, length), 0)
    col_index = lax.broadcasted_iota(jnp.int32, (length, length), 1)
    lower_mask = row_index >= col_index
    strict = row_index > col_index
    differ = cumulative[..., :, None] - cumulative[..., None, :]
    weights = jnp.where(lower_mask, jnp.exp(jnp.where(lower_mask, differ, 0.0)), 0.0)
    solve_weights = jnp.where(strict, weights * beta_gate[..., :, None], 0.0)
    growth = jnp.exp(cumulative)
    final_sum = cumulative[..., -1]
    key_scale = beta_gate * growth
    carry_scale = jnp.exp(final_sum[..., None] - cumulative)
    decay_total = jnp.exp(final_sum)
    weights, solve_weights, growth, key_scale, carry_scale, decay_total = (
        lax.optimization_barrier(
            (weights, solve_weights, growth, key_scale, carry_scale, decay_total)
        )
    )
    key_dots = jnp.einsum("...cd,...ed->...ce", keys_in, keys_in, precision=HIGH_PRECISION)
    strict_part = key_dots * solve_weights
    right_side = jnp.concatenate(
        [beta_gate[..., None] * values_in, key_scale[..., None] * keys_in], axis=-1
    )
    inverse = lower_inverse(strict_part, length)
    solved = jnp.einsum("...ce,...ed->...cd", inverse, right_side, precision=HIGH_PRECISION)
    head_width = values_in.shape[-1]
    update_part = solved[..., :head_width]
    write_part = solved[..., head_width:]
    attend = jnp.einsum("...cd,...ed->...ce", queries, keys_in, precision=HIGH_PRECISION) * weights
    carried_keys = carry_scale[..., None] * keys_in
    return (
        update_part,
        write_part,
        attend,
        growth[..., None] * queries,
        carried_keys,
        decay_total,
    )


def advance(current_state, incoming_value_rows, carried_keys, decay_total):
    return decay_total[..., None, None] * current_state + jnp.einsum(
        "...ck,...cv->...kv", carried_keys, incoming_value_rows, precision=HIGH_PRECISION
    )


def pair_update(passed_block_state, inputs):
    current_update, current_write, carried_now, decay_now = inputs
    target_values = jnp.concatenate([current_update, jnp.zeros_like(current_update)], axis=-1)
    incoming_value_rows = target_values - jnp.einsum(
        "zsg,zgj->zsj", current_write, passed_block_state, precision=HIGH_PRECISION
    )
    return advance(passed_block_state, incoming_value_rows, carried_now, decay_now)


def shifted(value, axis, steps):
    count = lax.axis_size(axis)
    return lax.ppermute(value, axis, [(source, source + steps) for source in range(count - steps)])


def incoming_state(pair, axis):
    count = lax.axis_size(axis)
    place = lax.axis_index(axis)
    state = pair[..., :HD]
    if count == 1:
        return jnp.zeros_like(state)
    width = 1
    while 2 * width < count:
        got = shifted(pair, axis, width)
        joined = jnp.einsum("hij,hjk->hik", pair[..., HD:], got, precision=FAST_PRECISION)
        joined = joined + jnp.concatenate([pair[..., :HD], jnp.zeros_like(state)], axis=-1)
        pair = jnp.where(place >= width, joined, pair)
        width *= 2
    previous = shifted(pair, axis, 1)
    result = previous[..., :HD]
    if width + 1 < count:
        far_state = shifted(pair[..., :HD], axis, width + 1)
        result = result + jnp.einsum(
            "hij,hjk->hik", previous[..., HD:], far_state, precision=FAST_PRECISION
        )
    return result


def step_pair(pair, inputs):
    return (pair_update(pair, inputs), pair)


def local(qkv_blocks, block_scales, gate_logits, conv_weight, decay_log, dt_bias, norm_gain):
    side = jnp.concatenate([jnp.repeat(block_scales, QB, axis=0), gate_logits], axis=-1)
    coded_share = lax.all_to_all(qkv_blocks, "inner", split_axis=1, concat_axis=0, tiled=True)
    side_share = lax.all_to_all(side, "inner", split_axis=1, concat_axis=0, tiled=True)
    gate_share = side_share[..., 4:]
    regrouped = dequantize(coded_share, side_share[..., :4])
    token_count = regrouped.shape[0]
    tail = CONV - 1
    previous = from_behind(regrouped[token_count - tail :], "outer", 1)
    body = convolve(regrouped, conv_weight, token_count - tail)
    head = convolve(jnp.concatenate([previous, regrouped[:tail]], axis=0), conv_weight, tail)
    mixed = jnp.concatenate([head, body], axis=0)
    queries, keys_in, values_in, beta_gate, log_decay = split_heads(
        mixed, gate_share, decay_log, dt_bias
    )
    update_part, write_part, attend, grown_query, carried_keys, decay_total = block_terms(
        queries, keys_in, values_in, beta_gate, log_decay
    )
    head_count = queries.shape[1]
    zero_state = jnp.zeros((head_count, HD, HD), jnp.float32)
    identity = jnp.broadcast_to(jnp.eye(HD, dtype=jnp.float32), (head_count, HD, HD))
    start_pair = jnp.concatenate([zero_state, identity], axis=-1)
    sequence = (update_part, write_part, carried_keys, decay_total)
    final_pair, start_pairs = lax.scan(step_pair, start_pair, sequence, unroll=True)
    incoming = incoming_state(final_pair, "outer")
    effective_query = grown_query - jnp.einsum(
        "...ce,...ek->...ck", attend, write_part, precision=HIGH_PRECISION
    )
    local_part = jnp.einsum(
        "...ce,...ev->...cv", attend, update_part, precision=HIGH_PRECISION
    )
    through_state = jnp.einsum(
        "...ck,...kj->...cj", effective_query, start_pairs, precision=HIGH_PRECISION
    )
    local_part = local_part + through_state[..., :HD]
    outputs = local_part + jnp.einsum(
        "bhck,hkv->bhcv", through_state[..., HD:], incoming, precision=HIGH_PRECISION
    )
    scaled = (
        outputs
        * lax.rsqrt(jnp.mean(outputs * outputs, axis=-1, keepdims=True) + EPS_NORM)
        * norm_gain
    )
    normed = scaled.astype(jnp.bfloat16)
    by_token = jnp.swapaxes(normed, 1, 2).reshape(token_count, head_count, HD)
    return lax.all_to_all(by_token, "inner", split_axis=0, concat_axis=1, tiled=True)


def solution(mesh):
    placed = (
        P(("outer", "inner"), None, None),
        P(("outer", "inner"), None, None),
        P(("outer", "inner"), None, None),
        P(None, "inner", None),
        P("inner"),
        P("inner"),
        P(),
    )
    return jax.shard_map(
        local,
        mesh=mesh,
        in_specs=placed,
        out_specs=P(("outer", "inner"), None, None),
        check_vma=False,
    )
```

```python
import jax
import jax.numpy as jnp
from jax import lax
from jax.sharding import PartitionSpec as P

HD = 128
BLOCK = 128
QB = 32
CONV = 4


HIGH_PRECISION = lax.Precision.HIGHEST
FAST_PRECISION = lax.Precision.HIGH
EPS_NORM = 1e-06


def from_behind(value, axis, steps):
    count = lax.axis_size(axis)
    leading, last = (max(0, -steps), min(count, count - steps))
    return lax.ppermute(value, axis, [(source, source + steps) for source in range(leading, last)])


def dequantize(blocks, per_token):
    channels = blocks.shape[2]
    quarter = channels // 4
    per_token = per_token.astype(jnp.float32)
    group = lax.broadcasted_iota(jnp.int32, (1, 1, channels), 2) // quarter
    spread = jnp.broadcast_to(per_token[..., 0:1], blocks.shape)
    for part in range(1, 4):
        spread = jnp.where(group == part, per_token[..., part : part + 1], spread)
    return blocks.astype(jnp.float32) * spread


def convolve(extended, conv_weight, token_count):
    summed = conv_weight[0] * extended[0:token_count]
    for offset in range(1, CONV):
        summed = summed + conv_weight[offset] * extended[offset : offset + token_count]
    return jax.nn.silu(summed)


def unit_rows(matrix):
    return matrix * lax.rsqrt(jnp.sum(matrix * matrix, axis=-1, keepdims=True) + EPS_NORM)


def split_heads(mixed, gate_share, decay_log, dt_bias):
    token_count = mixed.shape[0]
    value_heads = 2 * mixed.shape[1]
    block_count = token_count // BLOCK
    query_heads = unit_rows(mixed[:, :, :HD])
    key_heads = unit_rows(mixed[:, :, HD : 2 * HD])
    queries = jnp.repeat(query_heads, 2, axis=1)
    keys_in = jnp.repeat(key_heads, 2, axis=1)
    values_in = mixed[:, :, 2 * HD :].reshape(token_count, value_heads, HD)
    gate_values = gate_share.astype(jnp.float32)
    beta_gate = jax.nn.sigmoid(gate_values[:, :, :2].reshape(token_count, value_heads))
    raw_decay = gate_values[:, :, 2:].reshape(token_count, value_heads)
    log_decay = -jnp.exp(decay_log) * jax.nn.softplus(raw_decay + dt_bias)

    def blocked(tensor):
        return jnp.swapaxes(tensor.reshape((block_count, BLOCK) + tensor.shape[1:]), 1, 2)

    return (
        blocked(query_heads),
        blocked(key_heads),
        blocked(queries),
        blocked(keys_in),
        blocked(values_in),
        blocked(beta_gate),
        blocked(log_decay),
    )


def lower_inverse(strict_part, length):
    negated = -strict_part
    eye_block = jnp.eye(length, dtype=jnp.float32)
    inverse = eye_block + negated
    power = negated
    for unused_level in range((length - 1).bit_length() - 1):
        power = jnp.einsum("...ij,...jk->...ik", power, power, precision=FAST_PRECISION)
        inverse = inverse + jnp.einsum(
            "...ij,...jk->...ik", inverse, power, precision=FAST_PRECISION
        )
    return inverse


def block_terms(query_heads, key_heads, queries, keys_in, values_in, beta_gate, log_decay):
    cumulative = jnp.cumsum(log_decay, axis=-1)
    length = log_decay.shape[-1]
    row_index = lax.broadcasted_iota(jnp.int32, (length, length), 0)
    col_index = lax.broadcasted_iota(jnp.int32, (length, length), 1)
    lower_mask = row_index >= col_index
    strict = row_index > col_index
    differ = cumulative[..., :, None] - cumulative[..., None, :]
    weights = jnp.where(lower_mask, jnp.exp(jnp.where(lower_mask, differ, 0.0)), 0.0)
    solve_weights = jnp.where(strict, weights * beta_gate[..., :, None], 0.0)
    weights, solve_weights, cumulative = lax.optimization_barrier(
        (weights, solve_weights, cumulative)
    )
    key_dots = jnp.einsum("...cd,...ed->...ce", key_heads, key_heads, precision=HIGH_PRECISION)
    key_dots = jnp.repeat(key_dots, 2, axis=-3)
    strict_part = key_dots * solve_weights
    growth = jnp.exp(cumulative)
    right_side = jnp.concatenate(
        [beta_gate[..., None] * values_in, (beta_gate * growth)[..., None] * keys_in], axis=-1
    )
    inverse = lower_inverse(strict_part, length)
    solved = jnp.einsum("...ce,...ed->...cd", inverse, right_side, precision=HIGH_PRECISION)
    head_width = values_in.shape[-1]
    update_part = solved[..., :head_width]
    write_part = solved[..., head_width:]
    attend = jnp.einsum("...cd,...ed->...ce", query_heads, key_heads, precision=HIGH_PRECISION)
    attend = jnp.repeat(attend, 2, axis=-3) * weights
    final_sum = cumulative[..., -1]
    carried_keys = jnp.exp(final_sum[..., None] - cumulative)[..., None] * keys_in
    return (
        update_part,
        write_part,
        attend,
        growth[..., None] * queries,
        carried_keys,
        jnp.exp(final_sum),
    )


def advance(current_state, incoming_value_rows, carried_keys, decay_total):
    return decay_total[..., None, None] * current_state + jnp.einsum(
        "...ck,...cv->...kv", carried_keys, incoming_value_rows, precision=HIGH_PRECISION
    )


def pair_update(passed_block_state, inputs):
    current_update, current_write, carried_now, decay_now = inputs
    target_values = jnp.concatenate([current_update, jnp.zeros_like(current_update)], axis=-1)
    incoming_value_rows = target_values - jnp.einsum(
        "zsg,zgj->zsj", current_write, passed_block_state, precision=HIGH_PRECISION
    )
    return advance(passed_block_state, incoming_value_rows, carried_now, decay_now)


def shifted(value, axis, steps):
    count = lax.axis_size(axis)
    return lax.ppermute(value, axis, [(source, source + steps) for source in range(count - steps)])


def incoming_state(pair, axis):
    count = lax.axis_size(axis)
    place = lax.axis_index(axis)
    state = pair[..., :HD]
    if count == 1:
        return jnp.zeros_like(state)
    width = 1
    while 2 * width < count:
        got = shifted(pair, axis, width)
        joined = jnp.einsum("hij,hjk->hik", pair[..., HD:], got, precision=FAST_PRECISION)
        joined = joined + jnp.concatenate([pair[..., :HD], jnp.zeros_like(state)], axis=-1)
        pair = jnp.where(place >= width, joined, pair)
        width *= 2
    previous = shifted(pair, axis, 1)
    result = previous[..., :HD]
    if width + 1 < count:
        far_state = shifted(pair[..., :HD], axis, width + 1)
        result = result + jnp.einsum(
            "hij,hjk->hik", previous[..., HD:], far_state, precision=FAST_PRECISION
        )
    return result


def step_pair(pair, inputs):
    return (pair_update(pair, inputs), pair)


def local(qkv_blocks, block_scales, gate_logits, conv_weight, decay_log, dt_bias, norm_gain):
    side = jnp.concatenate([jnp.repeat(block_scales, QB, axis=0), gate_logits], axis=-1)
    coded_share = lax.all_to_all(qkv_blocks, "inner", split_axis=1, concat_axis=0, tiled=True)
    side_share = lax.all_to_all(side, "inner", split_axis=1, concat_axis=0, tiled=True)
    gate_share = side_share[..., 4:]
    regrouped = dequantize(coded_share, side_share[..., :4])
    token_count = regrouped.shape[0]
    tail = CONV - 1
    previous = from_behind(regrouped[token_count - tail :], "outer", 1)
    body = convolve(regrouped, conv_weight, token_count - tail)
    head = convolve(jnp.concatenate([previous, regrouped[:tail]], axis=0), conv_weight, tail)
    mixed = jnp.concatenate([head, body], axis=0)
    query_heads, key_heads, queries, keys_in, values_in, beta_gate, log_decay = split_heads(
        mixed, gate_share, decay_log, dt_bias
    )
    update_part, write_part, attend, grown_query, carried_keys, decay_total = block_terms(
        query_heads, key_heads, queries, keys_in, values_in, beta_gate, log_decay
    )
    head_count = queries.shape[1]
    zero_state = jnp.zeros((head_count, HD, HD), jnp.float32)
    identity = jnp.broadcast_to(jnp.eye(HD, dtype=jnp.float32), (head_count, HD, HD))
    start_pair = jnp.concatenate([zero_state, identity], axis=-1)
    sequence = (update_part, write_part, carried_keys, decay_total)
    final_pair, start_pairs = lax.scan(step_pair, start_pair, sequence, unroll=True)
    incoming = incoming_state(final_pair, "outer")
    effective_query = grown_query - jnp.einsum(
        "...ce,...ek->...ck", attend, write_part, precision=HIGH_PRECISION
    )
    local_part = jnp.einsum(
        "...ce,...ev->...cv", attend, update_part, precision=HIGH_PRECISION
    )
    through_state = jnp.einsum(
        "...ck,...kj->...cj", effective_query, start_pairs, precision=HIGH_PRECISION
    )
    local_part = local_part + through_state[..., :HD]
    outputs = local_part + jnp.einsum(
        "bhck,hkv->bhcv", through_state[..., HD:], incoming, precision=HIGH_PRECISION
    )
    scaled = (
        outputs
        * lax.rsqrt(jnp.mean(outputs * outputs, axis=-1, keepdims=True) + EPS_NORM)
        * norm_gain
    )
    normed = scaled.astype(jnp.bfloat16)
    by_token = jnp.swapaxes(normed, 1, 2).reshape(token_count, head_count, HD)
    return lax.all_to_all(by_token, "inner", split_axis=0, concat_axis=1, tiled=True)


def solution(mesh):
    placed = (
        P(("outer", "inner"), None, None),
        P(("outer", "inner"), None, None),
        P(("outer", "inner"), None, None),
        P(None, "inner", None),
        P("inner"),
        P("inner"),
        P(),
    )
    return jax.shard_map(
        local,
        mesh=mesh,
        in_specs=placed,
        out_specs=P(("outer", "inner"), None, None),
        check_vma=False,
    )
```
